256 devices in a mesh: seg: 128 (over y, x_hi, z, core), fsdp: 2 (over x_lo).
Axes of the slice: x: 4 (x_hi: 2, x_lo: 2; x = x_hi * 2 + x_lo), y: 4, z: 8, core: 2. Of those that a mesh axis runs over, the one named last changes fastest.
Arguments:
- hidden_states: bfloat16 [98304, 2048], P(('seg', 'fsdp'))
- queries: bfloat16 [98304, 2048], P(('seg', 'fsdp'))
- w_key: bfloat16 [2048, 2048], P('fsdp')
- w_value: bfloat16 [2048, 2048], P('fsdp'), may hold values from -0.125 to 0.125
Outputs:
- attended: bfloat16 [98304, 2048], P(('seg', 'fsdp'))
The draws below stay inside these ranges and needn't reach their ends.
All inputs are finite; a program needn't handle non-finite values.
Results may differ from the reference program's by a relative error of at most 0.0076.
Values may be sent and summed in bfloat16 or wider, within the bound.
No kernel may reach another device: no remote copies, remote signals or barrier semaphores. Data moves between devices by JAX's collectives and lax.ppermute only.
A program may use at most 128 MiB of HBM per device.

```python
import jax
import jax.numpy as jnp
from jax import lax

D = 2048
H = 16
HD = 128
MEM = 2
SEGLEN = 768
N_SEGS = 128
TOKENS = 98304


def hidden_values(key):
    base = jax.random.fold_in(key, 101)
    return jax.random.normal(base, (TOKENS, D), jnp.float32)


def key_weights(key):
    base = jax.random.fold_in(key, 201)
    return jax.random.normal(base, (D, H * HD), jnp.float32) * D ** (-0.5)


def draw_hidden_states(key, part):
    return hidden_values(key).astype(jnp.bfloat16)


def draw_w_key(key, part):
    return key_weights(key).astype(jnp.bfloat16)


def draw_queries(key, part):
    base = jax.random.fold_in(key, 401)
    return (2.0 * jax.random.normal(base, (TOKENS, H * HD), jnp.float32)).astype(jnp.bfloat16)


def levels(key, extent, pieces, smallest, largest):
    factor_of = 1.0
    for dim, parts in pieces:
        draws = jax.random.uniform(jax.random.fold_in(jax.random.fold_in(key, 6), dim), (parts,), jnp.float32, smallest / len(pieces), largest / len(pieces))
        factor_of = factor_of * jnp.repeat(jnp.exp(draws), extent[dim] // parts).reshape((-1,) + (1,) * (len(extent) - 1 - dim))
    return factor_of


def scatter_about(own_key, extent, scale, reach, cuts=(), kind=jnp.bfloat16):
    array = jax.random.normal(own_key, extent, jnp.float32) * scale
    if len(cuts) > 0:
        array = levels(own_key, extent, cuts, -0.22, 0.18) * array
    return jnp.clip(array, min=-reach, max=reach).astype(kind)


def setup_inputs(seed: int = 0) -> dict:
    seeds = jax.random.split(jax.random.key(seed), 5)
    return {
        "hidden_states": draw_hidden_states(jax.random.fold_in(seeds[4], 71), 0),
        "queries": draw_queries(jax.random.fold_in(seeds[4], 71), 0),
        "w_key": draw_w_key(jax.random.fold_in(seeds[4], 71), 0),
        "w_value": scatter_about(seeds[3], (D, H * HD), D ** -0.5, 0.125, ((0, 2),)),
    }


def attend_segment(query_rows, key_block, value_block, allowed):
    count = query_rows.shape[0]
    query_heads = query_rows.astype(jnp.float32).reshape(count, H, HD)
    key_heads = key_block.astype(jnp.float32).reshape(key_block.shape[0], H, HD)
    value_heads = value_block.astype(jnp.float32).reshape(value_block.shape[0], H, HD)
    scores = jnp.einsum("qhd,khd->hqk", query_heads, key_heads) * (HD ** -0.5)
    scores = jnp.where(allowed[None], scores, jnp.float32(-1e30))
    top_score = jnp.max(scores, axis=-1, keepdims=True)
    expo = jnp.where(allowed[None], jnp.exp(scores - top_score), jnp.float32(0.0))
    total = jnp.sum(expo, axis=-1)
    weights = lax.optimization_barrier(expo.astype(jnp.bfloat16)).astype(jnp.float32)
    mixed = jnp.einsum("hqk,khd->qhd", weights, value_heads)
    mixed = mixed / jnp.transpose(total)[:, :, None]
    return mixed.reshape(count, H * HD).astype(jnp.bfloat16)


def reference(hidden_states, queries, w_key, w_value):
    key_rows = jnp.dot(hidden_states, w_key, preferred_element_type=jnp.float32).astype(jnp.bfloat16)
    value_rows = jnp.dot(hidden_states, w_value, preferred_element_type=jnp.float32).astype(jnp.bfloat16)
    padding = jnp.zeros((MEM * SEGLEN, H * HD), jnp.bfloat16)
    key_padded = jnp.concatenate([padding, key_rows], axis=0)
    value_padded = jnp.concatenate([padding, value_rows], axis=0)
    key_pos = jnp.arange((MEM + 1) * SEGLEN, dtype=jnp.int32)
    block_of = key_pos // SEGLEN
    within = key_pos % SEGLEN
    query_pos = jnp.arange(SEGLEN, dtype=jnp.int32)

    def one_segment(seg_number):
        start = (seg_number * SEGLEN).astype(jnp.int32)
        key_block = lax.dynamic_slice_in_dim(key_padded, start, (MEM + 1) * SEGLEN, 0)
        value_block = lax.dynamic_slice_in_dim(value_padded, start, (MEM + 1) * SEGLEN, 0)
        query_rows = lax.dynamic_slice_in_dim(queries, start, SEGLEN, 0)
        earlier_ok = (block_of < MEM) & (seg_number >= MEM - block_of)
        own_ok = (block_of == MEM)[None, :] & (within[None, :] <= query_pos[:, None])
        allowed = earlier_ok[None, :] | own_ok
        return attend_segment(query_rows, key_block, value_block, allowed)

    result = lax.map(one_segment, jnp.arange(N_SEGS, dtype=jnp.int32))
    return result.reshape(TOKENS, H * HD)
```

```python
import jax
import jax.numpy as jnp
from jax import lax
from jax.sharding import PartitionSpec as P

HD = 128
MEM = 2
GROUP = 2


def from_behind(value, axis, steps):
    count = lax.axis_size(axis)
    leading, last = (max(0, -steps), min(count, count - steps))
    return lax.ppermute(value, axis, [(source, source + steps) for source in range(leading, last)])


def swap_halves(value):
    return lax.ppermute(value, "fsdp", [(0, 1), (1, 0)])


def in_order(first_is_mine, mine, other, axis):
    lead = jnp.where(first_is_mine, mine, other)
    tail = jnp.where(first_is_mine, other, mine)
    return jnp.concatenate([lead, tail], axis=axis)


def attend_group(query_rows, key_flat, value_flat, allowed, group_number):
    span = GROUP * HD
    count = query_rows.shape[0]
    query_part = lax.dynamic_slice_in_dim(query_rows, group_number * span, span, 1).reshape(
        count, GROUP, HD
    )
    key_part = lax.dynamic_slice_in_dim(key_flat, group_number * span, span, 1).reshape(
        key_flat.shape[0], GROUP, HD
    )
    value_part = lax.dynamic_slice_in_dim(value_flat, group_number * span, span, 1).reshape(
        value_flat.shape[0], GROUP, HD
    )
    scores = jnp.einsum(
        "qhd,khd->hqk", query_part, key_part, preferred_element_type=jnp.float32
    ) * HD ** (-0.5)
    scores = jnp.where(allowed[None], scores, jnp.float32(-1e30))
    top_score = jnp.max(scores, axis=-1, keepdims=True)
    expo = jnp.where(allowed[None], jnp.exp(scores - top_score), jnp.float32(0.0))
    total = jnp.sum(expo, axis=-1)
    weights = expo.astype(jnp.bfloat16)
    mixed = jnp.einsum("hqk,khd->qhd", weights, value_part, preferred_element_type=jnp.float32)
    mixed = mixed / jnp.transpose(total)[:, :, None]
    return mixed.reshape(count, span).astype(jnp.bfloat16)


def body(hidden_states, queries, w_key, w_value):
    tok_rows = hidden_states.shape[0]
    width = w_key.shape[1]
    halves = lax.axis_size("fsdp")
    cols = width // halves
    half_number = lax.axis_index("fsdp")
    other_half = 1 - half_number
    first_is_mine = half_number == 0

    def mine_of(array):
        return lax.dynamic_slice_in_dim(array, half_number * cols, cols, 1)

    def theirs_of(array):
        return lax.dynamic_slice_in_dim(array, other_half * cols, cols, 1)

    key_got = swap_halves(theirs_of(w_key))
    value_got = swap_halves(theirs_of(w_value))
    hidden_got = swap_halves(hidden_states)
    query_got = swap_halves(theirs_of(queries))

    key_weights = in_order(first_is_mine, mine_of(w_key), key_got, 0)
    value_weights = in_order(first_is_mine, mine_of(w_value), value_got, 0)
    hidden_rows = in_order(first_is_mine, hidden_states, hidden_got, 0)
    query_rows = in_order(first_is_mine, mine_of(queries), query_got, 0)

    own_key = jnp.dot(hidden_rows, key_weights, preferred_element_type=jnp.float32).astype(jnp.bfloat16)
    own_value = jnp.dot(hidden_rows, value_weights, preferred_element_type=jnp.float32).astype(
        jnp.bfloat16
    )
    own_unit = jnp.stack([own_key, own_value])
    earlier = []
    for distance in range(1, MEM + 1):
        earlier.insert(0, from_behind(own_unit, "seg", distance))
    context = jnp.stack(earlier + [own_unit])
    seg_rows = context.shape[2]
    key_flat = context[:, 0].reshape((MEM + 1) * seg_rows, cols)
    value_flat = context[:, 1].reshape((MEM + 1) * seg_rows, cols)
    seg_number = lax.axis_index("seg")
    query_pos = jnp.arange(seg_rows, dtype=jnp.int32)
    key_pos = jnp.arange((MEM + 1) * seg_rows, dtype=jnp.int32)
    block_of = key_pos // seg_rows
    within = key_pos % seg_rows
    earlier_ok = (block_of < MEM) & (seg_number >= MEM - block_of)
    own_ok = (block_of == MEM)[None, :] & (within[None, :] <= query_pos[:, None])
    allowed = earlier_ok[None, :] | own_ok

    def one_group(group_number):
        return attend_group(query_rows, key_flat, value_flat, allowed, group_number)

    grouped = lax.map(one_group, jnp.arange(cols // (GROUP * HD), dtype=jnp.int32))
    attended = jnp.transpose(grouped, (1, 0, 2)).reshape(seg_rows, cols)
    mine_rows = lax.dynamic_slice_in_dim(attended, half_number * tok_rows, tok_rows, 0)
    their_rows = lax.dynamic_slice_in_dim(attended, other_half * tok_rows, tok_rows, 0)
    rows_got = swap_halves(their_rows)
    return in_order(first_is_mine, mine_rows, rows_got, 1)


def solution(mesh):
    placed = (P(("seg", "fsdp"), None), P(("seg", "fsdp"), None), P("fsdp", None), P("fsdp", None))
    return jax.shard_map(
        body, mesh=mesh, in_specs=placed, out_specs=P(("seg", "fsdp"), None), check_vma=False
    )
```

```python
import functools

import jax
import jax.numpy as jnp
from jax import lax
from jax.experimental import pallas as pl
from jax.experimental.pallas import tpu as pltpu
from jax.sharding import PartitionSpec as P

HD = 128
MEM = 2
QBLOCK = 384
INTERPRET = False


def from_behind(value, axis, steps):
    count = lax.axis_size(axis)
    leading, last = (max(0, -steps), min(count, count - steps))
    return lax.ppermute(value, axis, [(source, source + steps) for source in range(leading, last)])


def swap_halves(value):
    return lax.ppermute(value, "fsdp", [(0, 1), (1, 0)])


def in_order(first_is_mine, mine, other, axis):
    lead = jnp.where(first_is_mine, mine, other)
    tail = jnp.where(first_is_mine, other, mine)
    return jnp.concatenate([lead, tail], axis=axis)


def attention_kernel(seg_ref, q_ref, k2_ref, k1_ref, k0_ref, v2_ref, v1_ref, v0_ref, o_ref):
    block = pl.program_id(1)
    seg = seg_ref[0]
    query = q_ref[...]
    seg_rows = k0_ref.shape[0]
    count = query.shape[0]
    dims = (((1,), (1,)), ((), ()))

    def scores_of(key_ref):
        raw = lax.dot_general(query, key_ref[...], dims, preferred_element_type=jnp.float32)
        return raw * HD ** (-0.5)

    col = lax.broadcasted_iota(jnp.int32, (count, seg_rows), 1)
    row = lax.broadcasted_iota(jnp.int32, (count, seg_rows), 0) + block * count
    ok2 = col < jnp.where(seg >= 2, seg_rows, 0)
    ok1 = col < jnp.where(seg >= 1, seg_rows, 0)
    ok0 = col <= row
    low = jnp.float32(-1e30)
    s2 = jnp.where(ok2, scores_of(k2_ref), low)
    s1 = jnp.where(ok1, scores_of(k1_ref), low)
    s0 = jnp.where(ok0, scores_of(k0_ref), low)
    top = jnp.maximum(
        jnp.maximum(jnp.max(s2, axis=1, keepdims=True), jnp.max(s1, axis=1, keepdims=True)),
        jnp.max(s0, axis=1, keepdims=True),
    )
    e2 = jnp.where(ok2, jnp.exp(s2 - top), 0.0)
    e1 = jnp.where(ok1, jnp.exp(s1 - top), 0.0)
    e0 = jnp.where(ok0, jnp.exp(s0 - top), 0.0)
    total = (
        jnp.sum(e2, axis=1, keepdims=True)
        + jnp.sum(e1, axis=1, keepdims=True)
        + jnp.sum(e0, axis=1, keepdims=True)
    )
    mixed = jnp.dot(e2.astype(jnp.bfloat16), v2_ref[...], preferred_element_type=jnp.float32)
    mixed = mixed + jnp.dot(e1.astype(jnp.bfloat16), v1_ref[...], preferred_element_type=jnp.float32)
    mixed = mixed + jnp.dot(e0.astype(jnp.bfloat16), v0_ref[...], preferred_element_type=jnp.float32)
    o_ref[...] = (mixed / total).astype(o_ref.dtype)


def attend(seg_number, query_rows, keys, values):
    seg_rows, cols = query_rows.shape
    heads = cols // HD
    blocks = seg_rows // QBLOCK
    q_spec = pl.BlockSpec((QBLOCK, HD), lambda h, i, seg: (i, h))
    kv_spec = pl.BlockSpec((seg_rows, HD), lambda h, i, seg: (0, h))
    grid_spec = pltpu.PrefetchScalarGridSpec(
        num_scalar_prefetch=1,
        grid=(heads, blocks),
        in_specs=[q_spec] + [kv_spec] * 6,
        out_specs=q_spec,
    )
    return pl.pallas_call(
        attention_kernel,
        grid_spec=grid_spec,
        out_shape=jax.ShapeDtypeStruct((seg_rows, cols), jnp.bfloat16),
        interpret=INTERPRET,
    )(seg_number.reshape(1).astype(jnp.int32), query_rows, *keys, *values)


def body(hidden_states, queries, w_key, w_value):
    tok_rows = hidden_states.shape[0]
    width = w_key.shape[1]
    halves = lax.axis_size("fsdp")
    segs = lax.axis_size("seg")
    cols = width // halves
    piece = cols // 2
    half_number = lax.axis_index("fsdp")
    seg_number = lax.axis_index("seg")
    other_half = 1 - half_number
    first_is_mine = half_number == 0
    core = seg_number % 2
    is_key_core = core == 0

    def mine_of(array):
        return lax.dynamic_slice_in_dim(array, half_number * cols, cols, 1)

    def theirs_of(array):
        return lax.dynamic_slice_in_dim(array, other_half * cols, cols, 1)

    served = jnp.where(is_key_core, theirs_of(w_key), theirs_of(w_value))
    left_got = swap_halves(served[:, :piece])
    stride = segs // 8 if segs >= 16 else 0
    wrap_pairs = []
    for seg in range(segs):
        for half in range(halves):
            wrap_pairs.append(((seg ^ stride) * halves + (1 - half), seg * halves + half))
    right_got = lax.ppermute(served[:, piece:], ("seg", "fsdp"), wrap_pairs)
    piece_got = jnp.concatenate([left_got, right_got], axis=1)
    core_pairs = [(seg, seg ^ 1) for seg in range(segs)]
    piece_other = lax.ppermute(piece_got, "seg", core_pairs)
    key_got = jnp.where(is_key_core, piece_got, piece_other)
    value_got = jnp.where(is_key_core, piece_other, piece_got)

    hidden_got = swap_halves(hidden_states)
    query_got = swap_halves(theirs_of(queries))

    key_weights = in_order(first_is_mine, mine_of(w_key), key_got, 0)
    value_weights = in_order(first_is_mine, mine_of(w_value), value_got, 0)
    hidden_rows = in_order(first_is_mine, hidden_states, hidden_got, 0)
    query_rows = in_order(first_is_mine, mine_of(queries), query_got, 0)

    own_key = jnp.dot(hidden_rows, key_weights, preferred_element_type=jnp.float32).astype(jnp.bfloat16)
    own_value = jnp.dot(hidden_rows, value_weights, preferred_element_type=jnp.float32).astype(
        jnp.bfloat16
    )
    own_unit = jnp.stack([own_key, own_value])
    one_back = from_behind(own_unit, "seg", 1)
    even_two = lax.ppermute(own_unit, "seg", [(s, s + 2) for s in range(0, segs - 2, 2)])
    odd_two = lax.ppermute(one_back, "seg", [(s, s + 1) for s in range(0, segs - 1, 2)])
    two_back = jnp.where(is_key_core, even_two, odd_two)

    attended = attend(
        seg_number,
        query_rows,
        (two_back[0], one_back[0], own_unit[0]),
        (two_back[1], one_back[1], own_unit[1]),
    )
    mine_rows = lax.dynamic_slice_in_dim(attended, half_number * tok_rows, tok_rows, 0)
    their_rows = lax.dynamic_slice_in_dim(attended, other_half * tok_rows, tok_rows, 0)
    rows_got = swap_halves(their_rows)
    return in_order(first_is_mine, mine_rows, rows_got, 1)


def solution(mesh):
    placed = (P(("seg", "fsdp"), None), P(("seg", "fsdp"), None), P("fsdp", None), P("fsdp", None))
    return jax.shard_map(
        body, mesh=mesh, in_specs=placed, out_specs=P(("seg", "fsdp"), None), check_vma=False
    )
```

```python
import functools

import jax
import jax.numpy as jnp
from jax import lax
from jax.experimental import pallas as pl
from jax.experimental.pallas import tpu as pltpu
from jax.sharding import PartitionSpec as P

HD = 128
MEM = 2
QBLOCK = 384
INTERPRET = False


def from_behind(value, axis, steps):
    count = lax.axis_size(axis)
    leading, last = (max(0, -steps), min(count, count - steps))
    return lax.ppermute(value, axis, [(source, source + steps) for source in range(leading, last)])


def swap_halves(value):
    return lax.ppermute(value, "fsdp", [(0, 1), (1, 0)])


def in_order(first_is_mine, mine, other, axis):
    lead = jnp.where(first_is_mine, mine, other)
    tail = jnp.where(first_is_mine, other, mine)
    return jnp.concatenate([lead, tail], axis=axis)


def attention_kernel(seg_ref, q_ref, k2_ref, k1_ref, k0_ref, v2_ref, v1_ref, v0_ref, o_ref):
    seg = seg_ref[0]
    first_row = seg_ref[1]
    query = q_ref[...]
    seg_rows = k0_ref.shape[0]
    count = query.shape[0]
    dims = (((1,), (1,)), ((), ()))

    def scores_of(key_ref):
        raw = lax.dot_general(query, key_ref[...], dims, preferred_element_type=jnp.float32)
        return raw * HD ** (-0.5)

    col = lax.broadcasted_iota(jnp.int32, (count, seg_rows), 1)
    row = lax.broadcasted_iota(jnp.int32, (count, seg_rows), 0) + first_row
    ok2 = col < jnp.where(seg >= 2, seg_rows, 0)
    ok1 = col < jnp.where(seg >= 1, seg_rows, 0)
    ok0 = col <= row
    low = jnp.float32(-1e30)
    s2 = jnp.where(ok2, scores_of(k2_ref), low)
    s1 = jnp.where(ok1, scores_of(k1_ref), low)
    s0 = jnp.where(ok0, scores_of(k0_ref), low)
    top = jnp.maximum(
        jnp.maximum(jnp.max(s2, axis=1, keepdims=True), jnp.max(s1, axis=1, keepdims=True)),
        jnp.max(s0, axis=1, keepdims=True),
    )
    e2 = jnp.where(ok2, jnp.exp(s2 - top), 0.0)
    e1 = jnp.where(ok1, jnp.exp(s1 - top), 0.0)
    e0 = jnp.where(ok0, jnp.exp(s0 - top), 0.0)
    total = (
        jnp.sum(e2, axis=1, keepdims=True)
        + jnp.sum(e1, axis=1, keepdims=True)
        + jnp.sum(e0, axis=1, keepdims=True)
    )
    mixed = jnp.dot(e2.astype(jnp.bfloat16), v2_ref[...], preferred_element_type=jnp.float32)
    mixed = mixed + jnp.dot(e1.astype(jnp.bfloat16), v1_ref[...], preferred_element_type=jnp.float32)
    mixed = mixed + jnp.dot(e0.astype(jnp.bfloat16), v0_ref[...], preferred_element_type=jnp.float32)
    o_ref[...] = (mixed / total).astype(o_ref.dtype)


def attend(seg_number, first_row, query_rows, keys, values):
    count, cols = query_rows.shape
    seg_rows = keys[0].shape[0]
    heads = cols // HD
    q_spec = pl.BlockSpec((count, HD), lambda h, scalars: (0, h))
    kv_spec = pl.BlockSpec((seg_rows, HD), lambda h, scalars: (0, h))
    grid_spec = pltpu.PrefetchScalarGridSpec(
        num_scalar_prefetch=1,
        grid=(heads,),
        in_specs=[q_spec] + [kv_spec] * 6,
        out_specs=q_spec,
    )
    scalars = jnp.stack([seg_number, first_row]).astype(jnp.int32)
    return pl.pallas_call(
        attention_kernel,
        grid_spec=grid_spec,
        out_shape=jax.ShapeDtypeStruct((count, cols), jnp.bfloat16),
        interpret=INTERPRET,
    )(scalars, query_rows, *keys, *values)


def body(hidden_states, queries, w_key, w_value):
    tok_rows = hidden_states.shape[0]
    width = w_key.shape[1]
    halves = lax.axis_size("fsdp")
    segs = lax.axis_size("seg")
    cols = width // halves
    piece = cols // 2
    half_number = lax.axis_index("fsdp")
    seg_number = lax.axis_index("seg")
    other_half = 1 - half_number
    first_is_mine = half_number == 0
    core = seg_number % 2
    is_key_core = core == 0

    def mine_of(array):
        return lax.dynamic_slice_in_dim(array, half_number * cols, cols, 1)

    def theirs_of(array):
        return lax.dynamic_slice_in_dim(array, other_half * cols, cols, 1)

    served = jnp.where(is_key_core, theirs_of(w_key), theirs_of(w_value))
    left_got = swap_halves(served[:, :piece])
    stride = segs // 8 if segs >= 16 else 0
    wrap_pairs = []
    for seg in range(segs):
        for half in range(halves):
            wrap_pairs.append(((seg ^ stride) * halves + (1 - half), seg * halves + half))
    right_got = lax.ppermute(served[:, piece:], ("seg", "fsdp"), wrap_pairs)
    piece_got = jnp.concatenate([left_got, right_got], axis=1)
    core_pairs = [(seg, seg ^ 1) for seg in range(segs)]
    piece_other = lax.ppermute(piece_got, "seg", core_pairs)
    key_got = jnp.where(is_key_core, piece_got, piece_other)
    value_got = jnp.where(is_key_core, piece_other, piece_got)

    hidden_got = swap_halves(hidden_states)

    key_weights = in_order(first_is_mine, mine_of(w_key), key_got, 0)
    value_weights = in_order(first_is_mine, mine_of(w_value), value_got, 0)
    hidden_rows = in_order(first_is_mine, hidden_states, hidden_got, 0)

    own_key = jnp.dot(hidden_rows, key_weights, preferred_element_type=jnp.float32).astype(jnp.bfloat16)
    own_value = jnp.dot(hidden_rows, value_weights, preferred_element_type=jnp.float32).astype(
        jnp.bfloat16
    )
    query_sent, own_key, own_value = lax.optimization_barrier((theirs_of(queries), own_key, own_value))
    query_got = swap_halves(query_sent)

    even_pairs = [(s, s + 2) for s in range(0, segs - 2, 2)]
    forward_pairs = [(s, s + 1) for s in range(0, segs - 1, 2)]

    def shifted(own):
        one = from_behind(own, "seg", 1)
        even_two = lax.ppermute(own, "seg", even_pairs)
        odd_two = lax.ppermute(one, "seg", forward_pairs)
        return jnp.where(is_key_core, even_two, odd_two), one

    key_two, key_one = shifted(own_key)
    value_two, value_one = shifted(own_value)
    keys = (key_two, key_one, own_key)
    values = (value_two, value_one, own_value)

    their_rows = attend(seg_number, other_half * tok_rows, query_got, keys, values)
    rows_got = swap_halves(their_rows)
    mine_rows = attend(seg_number, half_number * tok_rows, mine_of(queries), keys, values)
    return in_order(first_is_mine, mine_rows, rows_got, 1)


def solution(mesh):
    placed = (P(("seg", "fsdp"), None), P(("seg", "fsdp"), None), P("fsdp", None), P("fsdp", None))
    return jax.shard_map(
        body, mesh=mesh, in_specs=placed, out_specs=P(("seg", "fsdp"), None), check_vma=False
    )
```

```python
import functools

import jax
import jax.numpy as jnp
from jax import lax
from jax.experimental import pallas as pl
from jax.experimental.pallas import tpu as pltpu
from jax.sharding import PartitionSpec as P

HD = 128
MEM = 2
QBLOCK = 384
INTERPRET = False


def from_behind(value, axis, steps):
    count = lax.axis_size(axis)
    leading, last = (max(0, -steps), min(count, count - steps))
    return lax.ppermute(value, axis, [(source, source + steps) for source in range(leading, last)])


def swap_halves(value):
    return lax.ppermute(value, "fsdp", [(0, 1), (1, 0)])


def in_order(first_is_mine, mine, other, axis):
    lead = jnp.where(first_is_mine, mine, other)
    tail = jnp.where(first_is_mine, other, mine)
    return jnp.concatenate([lead, tail], axis=axis)


def attention_kernel(seg_ref, q_ref, k2_ref, k1_ref, k0_ref, v2_ref, v1_ref, v0_ref, o_ref):
    seg = seg_ref[0]
    first_row = seg_ref[1]
    query = q_ref[...]
    seg_rows = k0_ref.shape[0]
    count = query.shape[0]
    dims = (((1,), (1,)), ((), ()))

    def scores_of(key_ref):
        raw = lax.dot_general(query, key_ref[...], dims, preferred_element_type=jnp.float32)
        return raw * HD ** (-0.5)

    col = lax.broadcasted_iota(jnp.int32, (count, seg_rows), 1)
    row = lax.broadcasted_iota(jnp.int32, (count, seg_rows), 0) + first_row
    low = jnp.float32(-1e30)
    s0 = jnp.where(col <= row, scores_of(k0_ref), low)
    top0 = jnp.max(s0, axis=1, keepdims=True)

    def finish(s2, s1, e2_of, e1_of):
        top = jnp.maximum(
            jnp.maximum(jnp.max(s2, axis=1, keepdims=True), jnp.max(s1, axis=1, keepdims=True)), top0
        )
        e2 = e2_of(s2, top)
        e1 = e1_of(s1, top)
        e0 = jnp.where(col <= row, jnp.exp(s0 - top), 0.0)
        total = (
            jnp.sum(e2, axis=1, keepdims=True)
            + jnp.sum(e1, axis=1, keepdims=True)
            + jnp.sum(e0, axis=1, keepdims=True)
        )
        mixed = jnp.dot(e2.astype(jnp.bfloat16), v2_ref[...], preferred_element_type=jnp.float32)
        mixed = mixed + jnp.dot(e1.astype(jnp.bfloat16), v1_ref[...], preferred_element_type=jnp.float32)
        mixed = mixed + jnp.dot(e0.astype(jnp.bfloat16), v0_ref[...], preferred_element_type=jnp.float32)
        o_ref[...] = (mixed / total).astype(o_ref.dtype)

    @pl.when(seg >= MEM)
    def _():
        plain = lambda s, top: jnp.exp(s - top)
        finish(scores_of(k2_ref), scores_of(k1_ref), plain, plain)

    @pl.when(seg < MEM)
    def _():
        ok2 = col < jnp.where(seg >= 2, seg_rows, 0)
        ok1 = col < jnp.where(seg >= 1, seg_rows, 0)
        s2 = jnp.where(ok2, scores_of(k2_ref), low)
        s1 = jnp.where(ok1, scores_of(k1_ref), low)
        finish(
            s2,
            s1,
            lambda s, top: jnp.where(ok2, jnp.exp(s - top), 0.0),
            lambda s, top: jnp.where(ok1, jnp.exp(s - top), 0.0),
        )


def attend(seg_number, first_row, query_rows, keys, values, head_lo, head_count):
    count = query_rows.shape[0]
    seg_rows = keys[0].shape[0]
    q_spec = pl.BlockSpec((count, HD), lambda h, scalars: (0, h + head_lo))
    kv_spec = pl.BlockSpec((seg_rows, HD), lambda h, scalars: (0, h + head_lo))
    o_spec = pl.BlockSpec((count, HD), lambda h, scalars: (0, h))
    grid_spec = pltpu.PrefetchScalarGridSpec(
        num_scalar_prefetch=1,
        grid=(head_count,),
        in_specs=[q_spec] + [kv_spec] * 6,
        out_specs=o_spec,
    )
    scalars = jnp.stack([seg_number, first_row]).astype(jnp.int32)
    return pl.pallas_call(
        attention_kernel,
        grid_spec=grid_spec,
        out_shape=jax.ShapeDtypeStruct((count, head_count * HD), jnp.bfloat16),
        interpret=INTERPRET,
    )(scalars, query_rows, *keys, *values)


def body(hidden_states, queries, w_key, w_value):
    tok_rows = hidden_states.shape[0]
    width = w_key.shape[1]
    halves = lax.axis_size("fsdp")
    segs = lax.axis_size("seg")
    cols = width // halves
    piece = cols // 2
    half_number = lax.axis_index("fsdp")
    seg_number = lax.axis_index("seg")
    other_half = 1 - half_number
    first_is_mine = half_number == 0
    core = seg_number % 2
    is_key_core = core == 0

    def mine_of(array):
        return lax.dynamic_slice_in_dim(array, half_number * cols, cols, 1)

    def theirs_of(array):
        return lax.dynamic_slice_in_dim(array, other_half * cols, cols, 1)

    served = jnp.where(is_key_core, theirs_of(w_key), theirs_of(w_value))
    left_got = swap_halves(served[:, :piece])
    stride = segs // 8 if segs >= 16 else 0
    wrap_pairs = []
    for seg in range(segs):
        for half in range(halves):
            wrap_pairs.append(((seg ^ stride) * halves + (1 - half), seg * halves + half))
    right_got = lax.ppermute(served[:, piece:], ("seg", "fsdp"), wrap_pairs)
    piece_got = jnp.concatenate([left_got, right_got], axis=1)
    core_pairs = [(seg, seg ^ 1) for seg in range(segs)]
    piece_other = lax.ppermute(piece_got, "seg", core_pairs)
    key_got = jnp.where(is_key_core, piece_got, piece_other)
    value_got = jnp.where(is_key_core, piece_other, piece_got)

    hidden_got = swap_halves(hidden_states)

    key_weights = in_order(first_is_mine, mine_of(w_key), key_got, 0)
    value_weights = in_order(first_is_mine, mine_of(w_value), value_got, 0)
    hidden_rows = in_order(first_is_mine, hidden_states, hidden_got, 0)

    own_key = jnp.dot(hidden_rows, key_weights, preferred_element_type=jnp.float32).astype(jnp.bfloat16)
    own_value = jnp.dot(hidden_rows, value_weights, preferred_element_type=jnp.float32).astype(
        jnp.bfloat16
    )
    query_sent, own_key, own_value = lax.optimization_barrier((theirs_of(queries), own_key, own_value))
    query_got = swap_halves(query_sent)

    even_pairs = [(s, s + 2) for s in range(0, segs - 2, 2)]
    forward_pairs = [(s, s + 1) for s in range(0, segs - 1, 2)]

    def shifted(own):
        one = from_behind(own, "seg", 1)
        even_two = lax.ppermute(own, "seg", even_pairs)
        odd_two = lax.ppermute(one, "seg", forward_pairs)
        return jnp.where(is_key_core, even_two, odd_two), one

    key_two, key_one = shifted(own_key)
    value_two, value_one = shifted(own_value)
    keys = (key_two, key_one, own_key)
    values = (value_two, value_one, own_value)

    heads = cols // HD
    mine_rows = attend(seg_number, half_number * tok_rows, mine_of(queries), keys, values, 0, heads)
    query_got, mine_rows = lax.optimization_barrier((query_got, mine_rows))
    got = []
    for head_lo in range(0, heads, heads // 2):
        their_rows = attend(seg_number, other_half * tok_rows, query_got, keys, values, head_lo, heads // 2)
        got.append(swap_halves(their_rows))
    rows_got = jnp.concatenate(got, axis=1)
    return in_order(first_is_mine, mine_rows, rows_got, 1)


def solution(mesh):
    placed = (P(("seg", "fsdp"), None), P(("seg", "fsdp"), None), P("fsdp", None), P("fsdp", None))
    return jax.shard_map(
        body, mesh=mesh, in_specs=placed, out_specs=P(("seg", "fsdp"), None), check_vma=False
    )
```

```python
import functools

import jax
import jax.numpy as jnp
from jax import lax
from jax.experimental import pallas as pl
from jax.experimental.pallas import tpu as pltpu
from jax.sharding import PartitionSpec as P

HD = 128
MEM = 2
QBLOCK = 384
INTERPRET = False


def from_behind(value, axis, steps):
    count = lax.axis_size(axis)
    leading, last = (max(0, -steps), min(count, count - steps))
    return lax.ppermute(value, axis, [(source, source + steps) for source in range(leading, last)])


def swap_halves(value):
    return lax.ppermute(value, "fsdp", [(0, 1), (1, 0)])


def in_order(first_is_mine, mine, other, axis):
    lead = jnp.where(first_is_mine, mine, other)
    tail = jnp.where(first_is_mine, other, mine)
    return jnp.concatenate([lead, tail], axis=axis)


def attention_kernel(seg_ref, q_ref, k2_ref, k1_ref, k0_ref, v2_ref, v1_ref, v0_ref, o_ref):
    seg = seg_ref[0]
    first_row = seg_ref[1]
    query = q_ref[...]
    seg_rows = k0_ref.shape[0]
    count = query.shape[0]
    dims = (((1,), (1,)), ((), ()))

    def scores_of(key_ref):
        raw = lax.dot_general(query, key_ref[...], dims, preferred_element_type=jnp.float32)
        return raw * HD ** (-0.5)

    col = lax.broadcasted_iota(jnp.int32, (count, seg_rows), 1)
    row = lax.broadcasted_iota(jnp.int32, (count, seg_rows), 0) + first_row
    low = jnp.float32(-1e30)
    s0 = jnp.where(col <= row, scores_of(k0_ref), low)
    top0 = jnp.max(s0, axis=1, keepdims=True)

    def finish(s2, s1, e2_of, e1_of):
        top = jnp.maximum(
            jnp.maximum(jnp.max(s2, axis=1, keepdims=True), jnp.max(s1, axis=1, keepdims=True)), top0
        )
        e2 = e2_of(s2, top)
        e1 = e1_of(s1, top)
        e0 = jnp.where(col <= row, jnp.exp(s0 - top), 0.0)
        total = (
            jnp.sum(e2, axis=1, keepdims=True)
            + jnp.sum(e1, axis=1, keepdims=True)
            + jnp.sum(e0, axis=1, keepdims=True)
        )
        mixed = jnp.dot(e2.astype(jnp.bfloat16), v2_ref[...], preferred_element_type=jnp.float32)
        mixed = mixed + jnp.dot(e1.astype(jnp.bfloat16), v1_ref[...], preferred_element_type=jnp.float32)
        mixed = mixed + jnp.dot(e0.astype(jnp.bfloat16), v0_ref[...], preferred_element_type=jnp.float32)
        o_ref[...] = (mixed / total).astype(o_ref.dtype)

    @pl.when(seg >= MEM)
    def _():
        plain = lambda s, top: jnp.exp(s - top)
        finish(scores_of(k2_ref), scores_of(k1_ref), plain, plain)

    @pl.when(seg < MEM)
    def _():
        ok2 = col < jnp.where(seg >= 2, seg_rows, 0)
        ok1 = col < jnp.where(seg >= 1, seg_rows, 0)
        s2 = jnp.where(ok2, scores_of(k2_ref), low)
        s1 = jnp.where(ok1, scores_of(k1_ref), low)
        finish(
            s2,
            s1,
            lambda s, top: jnp.where(ok2, jnp.exp(s - top), 0.0),
            lambda s, top: jnp.where(ok1, jnp.exp(s - top), 0.0),
        )


def attend(seg_number, first_row, query_rows, keys, values, head_lo, head_count):
    count = query_rows.shape[0]
    seg_rows = keys[0].shape[0]
    q_spec = pl.BlockSpec((count, HD), lambda h, scalars: (0, h + head_lo))
    kv_spec = pl.BlockSpec((seg_rows, HD), lambda h, scalars: (0, h + head_lo))
    o_spec = pl.BlockSpec((count, HD), lambda h, scalars: (0, h))
    grid_spec = pltpu.PrefetchScalarGridSpec(
        num_scalar_prefetch=1,
        grid=(head_count,),
        in_specs=[q_spec] + [kv_spec] * 6,
        out_specs=o_spec,
    )
    scalars = jnp.stack([seg_number, first_row]).astype(jnp.int32)
    return pl.pallas_call(
        attention_kernel,
        grid_spec=grid_spec,
        out_shape=jax.ShapeDtypeStruct((count, head_count * HD), jnp.bfloat16),
        interpret=INTERPRET,
    )(scalars, query_rows, *keys, *values)


def body(hidden_states, queries, w_key, w_value):
    tok_rows = hidden_states.shape[0]
    width = w_key.shape[1]
    halves = lax.axis_size("fsdp")
    segs = lax.axis_size("seg")
    cols = width // halves
    piece = cols // 2
    half_number = lax.axis_index("fsdp")
    seg_number = lax.axis_index("seg")
    other_half = 1 - half_number
    first_is_mine = half_number == 0
    core = seg_number % 2
    is_key_core = core == 0

    def mine_of(array):
        return lax.dynamic_slice_in_dim(array, half_number * cols, cols, 1)

    def theirs_of(array):
        return lax.dynamic_slice_in_dim(array, other_half * cols, cols, 1)

    served = jnp.where(is_key_core, theirs_of(w_key), theirs_of(w_value))
    left_got = swap_halves(served[:, :piece])
    stride = segs // 8 if segs >= 16 else 0
    wrap_pairs = []
    for seg in range(segs):
        for half in range(halves):
            wrap_pairs.append(((seg ^ stride) * halves + (1 - half), seg * halves + half))
    right_got = lax.ppermute(served[:, piece:], ("seg", "fsdp"), wrap_pairs)
    hidden_sent, left_got, right_got = lax.optimization_barrier((hidden_states, left_got, right_got))
    hidden_got = swap_halves(hidden_sent)
    piece_got = jnp.concatenate([left_got, right_got], axis=1)
    core_pairs = [(seg, seg ^ 1) for seg in range(segs)]
    piece_other = lax.ppermute(piece_got, "seg", core_pairs)
    key_got = jnp.where(is_key_core, piece_got, piece_other)
    value_got = jnp.where(is_key_core, piece_other, piece_got)


    key_weights = in_order(first_is_mine, mine_of(w_key), key_got, 0)
    value_weights = in_order(first_is_mine, mine_of(w_value), value_got, 0)

    def project(rows):
        key = jnp.dot(rows, key_weights, preferred_element_type=jnp.float32).astype(jnp.bfloat16)
        value = jnp.dot(rows, value_weights, preferred_element_type=jnp.float32).astype(jnp.bfloat16)
        return jnp.stack([key, value])

    even_pairs = [(s, s + 2) for s in range(0, segs - 2, 2)]
    forward_pairs = [(s, s + 1) for s in range(0, segs - 1, 2)]

    def shifted(own):
        one = from_behind(own, "seg", 1)
        even_two = lax.ppermute(own, "seg", even_pairs)
        odd_two = lax.ppermute(one, "seg", forward_pairs)
        return jnp.where(is_key_core, even_two, odd_two), one

    mine_unit = project(hidden_states)
    mine_two, mine_one = shifted(mine_unit)
    hidden_got, mine_one = lax.optimization_barrier((hidden_got, mine_one))
    their_unit = project(hidden_got)
    query_sent, their_unit = lax.optimization_barrier((theirs_of(queries), their_unit))
    query_got = swap_halves(query_sent)
    their_two, their_one = shifted(their_unit)

    def whole(mine, theirs, part):
        return in_order(first_is_mine, mine[part], theirs[part], 0)

    keys = tuple(whole(m, t, 0) for m, t in ((mine_two, their_two), (mine_one, their_one), (mine_unit, their_unit)))
    values = tuple(whole(m, t, 1) for m, t in ((mine_two, their_two), (mine_one, their_one), (mine_unit, their_unit)))

    heads = cols // HD
    mine_rows = attend(seg_number, half_number * tok_rows, mine_of(queries), keys, values, 0, heads)
    query_got, mine_rows = lax.optimization_barrier((query_got, mine_rows))
    got = []
    for head_lo in range(0, heads, heads // 2):
        their_rows = attend(seg_number, other_half * tok_rows, query_got, keys, values, head_lo, heads // 2)
        got.append(swap_halves(their_rows))
    rows_got = jnp.concatenate(got, axis=1)
    return in_order(first_is_mine, mine_rows, rows_got, 1)


def solution(mesh):
    placed = (P(("seg", "fsdp"), None), P(("seg", "fsdp"), None), P("fsdp", None), P("fsdp", None))
    return jax.shard_map(
        body, mesh=mesh, in_specs=placed, out_specs=P(("seg", "fsdp"), None), check_vma=False
    )
```

```python
import functools

import jax
import jax.numpy as jnp
from jax import lax
from jax.experimental import pallas as pl
from jax.experimental.pallas import tpu as pltpu
from jax.sharding import PartitionSpec as P

HD = 128
MEM = 2
QBLOCK = 384
INTERPRET = False


def from_behind(value, axis, steps):
    count = lax.axis_size(axis)
    leading, last = (max(0, -steps), min(count, count - steps))
    return lax.ppermute(value, axis, [(source, source + steps) for source in range(leading, last)])


def swap_halves(value):
    return lax.ppermute(value, "fsdp", [(0, 1), (1, 0)])


def in_order(first_is_mine, mine, other, axis):
    lead = jnp.where(first_is_mine, mine, other)
    tail = jnp.where(first_is_mine, other, mine)
    return jnp.concatenate([lead, tail], axis=axis)


def attention_kernel(seg_ref, q_ref, k2_ref, k1_ref, k0_ref, v2_ref, v1_ref, v0_ref, o_ref):
    seg = seg_ref[0]
    first_row = seg_ref[1]
    count = q_ref.shape[0]
    seg_rows = k0_ref.shape[0]
    dims = (((1,), (1,)), ((), ()))
    low = jnp.float32(-1e30)

    def one_head(lanes, masked, own_rows):
        query = q_ref[:, lanes]

        def scores_of(key):
            raw = lax.dot_general(query, key, dims, preferred_element_type=jnp.float32)
            return raw * HD ** (-0.5)

        own_col = lax.broadcasted_iota(jnp.int32, (count, own_rows), 1)
        own_row = lax.broadcasted_iota(jnp.int32, (count, own_rows), 0) + first_row
        causal = own_col <= own_row
        s0 = jnp.where(causal, scores_of(k0_ref[:own_rows, lanes]), low)
        s2 = scores_of(k2_ref[:, lanes])
        s1 = scores_of(k1_ref[:, lanes])
        if masked:
            col = lax.broadcasted_iota(jnp.int32, (count, seg_rows), 1)
            ok2 = col < jnp.where(seg >= 2, seg_rows, 0)
            ok1 = col < jnp.where(seg >= 1, seg_rows, 0)
            s2 = jnp.where(ok2, s2, low)
            s1 = jnp.where(ok1, s1, low)
        top = jnp.maximum(
            jnp.maximum(jnp.max(s2, axis=1, keepdims=True), jnp.max(s1, axis=1, keepdims=True)),
            jnp.max(s0, axis=1, keepdims=True),
        )
        e2 = jnp.exp(s2 - top)
        e1 = jnp.exp(s1 - top)
        if masked:
            e2 = jnp.where(ok2, e2, 0.0)
            e1 = jnp.where(ok1, e1, 0.0)
        e0 = jnp.where(causal, jnp.exp(s0 - top), 0.0)
        total = (
            jnp.sum(e2, axis=1, keepdims=True)
            + jnp.sum(e1, axis=1, keepdims=True)
            + jnp.sum(e0, axis=1, keepdims=True)
        )
        mixed = jnp.dot(e2.astype(jnp.bfloat16), v2_ref[:, lanes], preferred_element_type=jnp.float32)
        mixed = mixed + jnp.dot(e1.astype(jnp.bfloat16), v1_ref[:, lanes], preferred_element_type=jnp.float32)
        mixed = mixed + jnp.dot(
            e0.astype(jnp.bfloat16), v0_ref[:own_rows, lanes], preferred_element_type=jnp.float32
        )
        o_ref[:, lanes] = (mixed / total).astype(o_ref.dtype)

    def run(masked, own_rows):
        for head in range(q_ref.shape[1] // HD):
            one_head(slice(head * HD, (head + 1) * HD), masked, own_rows)

    early = first_row + count <= count

    @pl.when(early)
    def _():
        run(True, count)

    @pl.when(jnp.logical_not(early))
    def _():
        run(True, seg_rows)


def attend(seg_number, first_row, query_rows, keys, values, head_lo, head_count):
    count = query_rows.shape[0]
    seg_rows = keys[0].shape[0]
    step = 1
    width = step * HD
    q_spec = pl.BlockSpec((count, width), lambda h, scalars: (0, h + head_lo // step))
    kv_spec = pl.BlockSpec((seg_rows, width), lambda h, scalars: (0, h + head_lo // step))
    o_spec = pl.BlockSpec((count, width), lambda h, scalars: (0, h))
    grid_spec = pltpu.PrefetchScalarGridSpec(
        num_scalar_prefetch=1,
        grid=(head_count // step,),
        in_specs=[q_spec] + [kv_spec] * 6,
        out_specs=o_spec,
    )
    scalars = jnp.stack([seg_number, first_row]).astype(jnp.int32)
    return pl.pallas_call(
        attention_kernel,
        grid_spec=grid_spec,
        out_shape=jax.ShapeDtypeStruct((count, head_count * HD), jnp.bfloat16),
        interpret=INTERPRET,
    )(scalars, query_rows, *keys, *values)


def body(hidden_states, queries, w_key, w_value):
    tok_rows = hidden_states.shape[0]
    width = w_key.shape[1]
    halves = lax.axis_size("fsdp")
    segs = lax.axis_size("seg")
    cols = width // halves
    piece = cols // 2
    half_number = lax.axis_index("fsdp")
    seg_number = lax.axis_index("seg")
    other_half = 1 - half_number
    first_is_mine = half_number == 0
    core = seg_number % 2
    is_key_core = core == 0

    def mine_of(array):
        return lax.dynamic_slice_in_dim(array, half_number * cols, cols, 1)

    def theirs_of(array):
        return lax.dynamic_slice_in_dim(array, other_half * cols, cols, 1)

    served = jnp.where(is_key_core, theirs_of(w_key), theirs_of(w_value))
    left_got = swap_halves(served[:, :piece])
    stride = segs // 8 if segs >= 16 else 0
    wrap_pairs = []
    for seg in range(segs):
        for half in range(halves):
            wrap_pairs.append(((seg ^ stride) * halves + (1 - half), seg * halves + half))
    right_got = lax.ppermute(served[:, piece:], ("seg", "fsdp"), wrap_pairs)
    piece_got = jnp.concatenate([left_got, right_got], axis=1)
    core_pairs = [(seg, seg ^ 1) for seg in range(segs)]
    piece_other = lax.ppermute(piece_got, "seg", core_pairs)
    key_got = jnp.where(is_key_core, piece_got, piece_other)
    value_got = jnp.where(is_key_core, piece_other, piece_got)

    hidden_got = swap_halves(hidden_states)

    key_weights = in_order(first_is_mine, mine_of(w_key), key_got, 0)
    value_weights = in_order(first_is_mine, mine_of(w_value), value_got, 0)
    hidden_rows = in_order(first_is_mine, hidden_states, hidden_got, 0)

    own_key = jnp.dot(hidden_rows, key_weights, preferred_element_type=jnp.float32).astype(jnp.bfloat16)
    own_value = jnp.dot(hidden_rows, value_weights, preferred_element_type=jnp.float32).astype(
        jnp.bfloat16
    )
    query_sent, own_key, own_value = lax.optimization_barrier((theirs_of(queries), own_key, own_value))
    query_got = swap_halves(query_sent)

    even_pairs = [(s, s + 2) for s in range(0, segs - 2, 2)]
    forward_pairs = [(s, s + 1) for s in range(0, segs - 1, 2)]

    def shifted(own):
        one = from_behind(own, "seg", 1)
        even_two = lax.ppermute(own, "seg", even_pairs)
        odd_two = lax.ppermute(one, "seg", forward_pairs)
        return jnp.where(is_key_core, even_two, odd_two), one

    key_two, key_one = shifted(own_key)
    value_two, value_one = shifted(own_value)
    keys = (key_two, key_one, own_key)
    values = (value_two, value_one, own_value)

    heads = cols // HD
    mine_rows = attend(seg_number, half_number * tok_rows, mine_of(queries), keys, values, 0, heads)
    query_got, mine_rows = lax.optimization_barrier((query_got, mine_rows))
    got = []
    lead = heads - heads // 4
    for head_lo, head_count in ((0, lead), (lead, heads - lead)):
        their_rows = attend(seg_number, other_half * tok_rows, query_got, keys, values, head_lo, head_count)
        got.append(swap_halves(their_rows))
    rows_got = jnp.concatenate(got, axis=1)
    return in_order(first_is_mine, mine_rows, rows_got, 1)


def solution(mesh):
    placed = (P(("seg", "fsdp"), None), P(("seg", "fsdp"), None), P("fsdp", None), P("fsdp", None))
    return jax.shard_map(
        body, mesh=mesh, in_specs=placed, out_specs=P(("seg", "fsdp"), None), check_vma=False
    )
```

```python
import functools

import jax
import jax.numpy as jnp
from jax import lax
from jax.experimental import pallas as pl
from jax.experimental.pallas import tpu as pltpu
from jax.sharding import PartitionSpec as P

HD = 128
MEM = 2
QBLOCK = 384
INTERPRET = False


def from_behind(value, axis, steps):
    count = lax.axis_size(axis)
    leading, last = (max(0, -steps), min(count, count - steps))
    return lax.ppermute(value, axis, [(source, source + steps) for source in range(leading, last)])


def swap_halves(value):
    return lax.ppermute(value, "fsdp", [(0, 1), (1, 0)])


def in_order(first_is_mine, mine, other, axis):
    lead = jnp.where(first_is_mine, mine, other)
    tail = jnp.where(first_is_mine, other, mine)
    return jnp.concatenate([lead, tail], axis=axis)


def attention_kernel(seg_ref, q_ref, k2_ref, k1_ref, k0_ref, v2_ref, v1_ref, v0_ref, o_ref):
    seg = seg_ref[0]
    first_row = seg_ref[1]
    count = q_ref.shape[0]
    seg_rows = k0_ref.shape[0]
    dims = (((1,), (1,)), ((), ()))
    low = jnp.float32(-1e30)

    def one_head(lanes, masked, own_rows):
        query = q_ref[:, lanes]

        def scores_of(key):
            raw = lax.dot_general(query, key, dims, preferred_element_type=jnp.float32)
            return raw * HD ** (-0.5)

        own_col = lax.broadcasted_iota(jnp.int32, (count, own_rows), 1)
        own_row = lax.broadcasted_iota(jnp.int32, (count, own_rows), 0) + first_row
        causal = own_col <= own_row
        s0 = jnp.where(causal, scores_of(k0_ref[:own_rows, lanes]), low)
        s2 = scores_of(k2_ref[:, lanes])
        s1 = scores_of(k1_ref[:, lanes])
        if masked:
            col = lax.broadcasted_iota(jnp.int32, (count, seg_rows), 1)
            ok2 = col < jnp.where(seg >= 2, seg_rows, 0)
            ok1 = col < jnp.where(seg >= 1, seg_rows, 0)
            s2 = jnp.where(ok2, s2, low)
            s1 = jnp.where(ok1, s1, low)
        top = jnp.maximum(
            jnp.maximum(jnp.max(s2, axis=1, keepdims=True), jnp.max(s1, axis=1, keepdims=True)),
            jnp.max(s0, axis=1, keepdims=True),
        )
        e2 = jnp.exp(s2 - top)
        e1 = jnp.exp(s1 - top)
        if masked:
            e2 = jnp.where(ok2, e2, 0.0)
            e1 = jnp.where(ok1, e1, 0.0)
        e0 = jnp.where(causal, jnp.exp(s0 - top), 0.0)
        total = (
            jnp.sum(e2, axis=1, keepdims=True)
            + jnp.sum(e1, axis=1, keepdims=True)
            + jnp.sum(e0, axis=1, keepdims=True)
        )
        mixed = jnp.dot(e2.astype(jnp.bfloat16), v2_ref[:, lanes], preferred_element_type=jnp.float32)
        mixed = mixed + jnp.dot(e1.astype(jnp.bfloat16), v1_ref[:, lanes], preferred_element_type=jnp.float32)
        mixed = mixed + jnp.dot(
            e0.astype(jnp.bfloat16), v0_ref[:own_rows, lanes], preferred_element_type=jnp.float32
        )
        o_ref[:, lanes] = (mixed / total).astype(o_ref.dtype)

    def run(masked, own_rows):
        for head in range(q_ref.shape[1] // HD):
            one_head(slice(head * HD, (head + 1) * HD), masked, own_rows)

    early = first_row + count <= count

    @pl.when(early)
    def _():
        run(True, count)

    @pl.when(jnp.logical_not(early))
    def _():
        run(True, seg_rows)


def attend(seg_number, first_row, query_rows, keys, values, head_lo, head_count):
    count = query_rows.shape[0]
    seg_rows = keys[0].shape[0]
    step = 1
    width = step * HD
    q_spec = pl.BlockSpec((count, width), lambda h, scalars: (0, h + head_lo // step))
    kv_spec = pl.BlockSpec((seg_rows, width), lambda h, scalars: (0, h + head_lo // step))
    o_spec = pl.BlockSpec((count, width), lambda h, scalars: (0, h))
    grid_spec = pltpu.PrefetchScalarGridSpec(
        num_scalar_prefetch=1,
        grid=(head_count // step,),
        in_specs=[q_spec] + [kv_spec] * 6,
        out_specs=o_spec,
    )
    scalars = jnp.stack([seg_number, first_row]).astype(jnp.int32)
    return pl.pallas_call(
        attention_kernel,
        grid_spec=grid_spec,
        out_shape=jax.ShapeDtypeStruct((count, head_count * HD), jnp.bfloat16),
        interpret=INTERPRET,
    )(scalars, query_rows, *keys, *values)


def body(hidden_states, queries, w_key, w_value):
    tok_rows = hidden_states.shape[0]
    width = w_key.shape[1]
    halves = lax.axis_size("fsdp")
    segs = lax.axis_size("seg")
    cols = width // halves
    piece = cols // 2
    half_number = lax.axis_index("fsdp")
    seg_number = lax.axis_index("seg")
    other_half = 1 - half_number
    first_is_mine = half_number == 0
    core = seg_number % 2
    is_key_core = core == 0

    def mine_of(array):
        return lax.dynamic_slice_in_dim(array, half_number * cols, cols, 1)

    def theirs_of(array):
        return lax.dynamic_slice_in_dim(array, other_half * cols, cols, 1)

    served = jnp.where(is_key_core, theirs_of(w_key), theirs_of(w_value))
    left_got = swap_halves(served[:, :piece])
    stride = segs // 8 if segs >= 16 else 0
    wrap_pairs = []
    for seg in range(segs):
        for half in range(halves):
            wrap_pairs.append(((seg ^ stride) * halves + (1 - half), seg * halves + half))
    right_got = lax.ppermute(served[:, piece:], ("seg", "fsdp"), wrap_pairs)
    piece_got = jnp.concatenate([left_got, right_got], axis=1)
    core_pairs = [(seg, seg ^ 1) for seg in range(segs)]
    piece_other = lax.ppermute(piece_got, "seg", core_pairs)
    key_got = jnp.where(is_key_core, piece_got, piece_other)
    value_got = jnp.where(is_key_core, piece_other, piece_got)

    hidden_got = swap_halves(hidden_states)

    key_weights = in_order(first_is_mine, mine_of(w_key), key_got, 0)
    value_weights = in_order(first_is_mine, mine_of(w_value), value_got, 0)
    hidden_rows = in_order(first_is_mine, hidden_states, hidden_got, 0)

    own_key = jnp.dot(hidden_rows, key_weights, preferred_element_type=jnp.float32).astype(jnp.bfloat16)
    own_value = jnp.dot(hidden_rows, value_weights, preferred_element_type=jnp.float32).astype(
        jnp.bfloat16
    )
    query_sent, own_key, own_value = lax.optimization_barrier((theirs_of(queries), own_key, own_value))
    query_got = swap_halves(query_sent)

    even_pairs = [(s, s + 2) for s in range(0, segs - 2, 2)]
    forward_pairs = [(s, s + 1) for s in range(0, segs - 1, 2)]

    def shifted(own):
        one = from_behind(own, "seg", 1)
        even_two = lax.ppermute(own, "seg", even_pairs)
        odd_two = lax.ppermute(one, "seg", forward_pairs)
        return jnp.where(is_key_core, even_two, odd_two), one

    key_two, key_one = shifted(own_key)
    value_two, value_one = shifted(own_value)
    keys = (key_two, key_one, own_key)
    values = (value_two, value_one, own_value)

    heads = cols // HD
    lead = heads - heads // 4
    mine_q = mine_of(queries)
    mine_lead = attend(seg_number, half_number * tok_rows, mine_q, keys, values, 0, lead)
    query_got, mine_lead = lax.optimization_barrier((query_got, mine_lead))
    got = []
    for head_lo in range(0, heads, heads // 2):
        their_rows = attend(seg_number, other_half * tok_rows, query_got, keys, values, head_lo, heads // 2)
        got.append(swap_halves(their_rows))
    mine_q, their_rows = lax.optimization_barrier((mine_q, their_rows))
    mine_tail = attend(seg_number, half_number * tok_rows, mine_q, keys, values, lead, heads - lead)
    mine_rows = jnp.concatenate([mine_lead, mine_tail], axis=1)
    rows_got = jnp.concatenate(got, axis=1)
    return in_order(first_is_mine, mine_rows, rows_got, 1)


def solution(mesh):
    placed = (P(("seg", "fsdp"), None), P(("seg", "fsdp"), None), P("fsdp", None), P("fsdp", None))
    return jax.shard_map(
        body, mesh=mesh, in_specs=placed, out_specs=P(("seg", "fsdp"), None), check_vma=False
    )
```

```python
import functools

import jax
import jax.numpy as jnp
from jax import lax
from jax.experimental import pallas as pl
from jax.experimental.pallas import tpu as pltpu
from jax.sharding import PartitionSpec as P

HD = 128
MEM = 2
QBLOCK = 384
INTERPRET = False


def from_behind(value, axis, steps):
    count = lax.axis_size(axis)
    leading, last = (max(0, -steps), min(count, count - steps))
    return lax.ppermute(value, axis, [(source, source + steps) for source in range(leading, last)])


def swap_halves(value):
    return lax.ppermute(value, "fsdp", [(0, 1), (1, 0)])


def in_order(first_is_mine, mine, other, axis):
    lead = jnp.where(first_is_mine, mine, other)
    tail = jnp.where(first_is_mine, other, mine)
    return jnp.concatenate([lead, tail], axis=axis)


def attention_kernel(
    seg_ref, q_ref, k2e_ref, k2o_ref, k1_ref, k0_ref, v2e_ref, v2o_ref, v1_ref, v0_ref, o_ref
):
    seg = seg_ref[0]
    first_row = seg_ref[1]
    even = seg_ref[2]
    count = q_ref.shape[0]
    seg_rows = k0_ref.shape[0]
    dims = (((1,), (1,)), ((), ()))
    low = jnp.float32(-1e30)

    def one_head(lanes, masked, own_rows):
        query = q_ref[:, lanes]

        def scores_of(key):
            raw = lax.dot_general(query, key, dims, preferred_element_type=jnp.float32)
            return raw * HD ** (-0.5)

        own_col = lax.broadcasted_iota(jnp.int32, (count, own_rows), 1)
        own_row = lax.broadcasted_iota(jnp.int32, (count, own_rows), 0) + first_row
        causal = own_col <= own_row
        s0 = jnp.where(causal, scores_of(k0_ref[:own_rows, lanes]), low)
        pick = lax.broadcasted_iota(jnp.int32, (seg_rows, HD), 0) < even * seg_rows
        s2 = scores_of(jnp.where(pick, k2e_ref[:, lanes], k2o_ref[:, lanes]))
        s1 = scores_of(k1_ref[:, lanes])
        if masked:
            col = lax.broadcasted_iota(jnp.int32, (count, seg_rows), 1)
            ok2 = col < jnp.where(seg >= 2, seg_rows, 0)
            ok1 = col < jnp.where(seg >= 1, seg_rows, 0)
            s2 = jnp.where(ok2, s2, low)
            s1 = jnp.where(ok1, s1, low)
        top = jnp.maximum(
            jnp.maximum(jnp.max(s2, axis=1, keepdims=True), jnp.max(s1, axis=1, keepdims=True)),
            jnp.max(s0, axis=1, keepdims=True),
        )
        e2 = jnp.exp(s2 - top)
        e1 = jnp.exp(s1 - top)
        if masked:
            e2 = jnp.where(ok2, e2, 0.0)
            e1 = jnp.where(ok1, e1, 0.0)
        e0 = jnp.where(causal, jnp.exp(s0 - top), 0.0)
        total = (
            jnp.sum(e2, axis=1, keepdims=True)
            + jnp.sum(e1, axis=1, keepdims=True)
            + jnp.sum(e0, axis=1, keepdims=True)
        )
        value2 = jnp.where(pick, v2e_ref[:, lanes], v2o_ref[:, lanes])
        mixed = jnp.dot(e2.astype(jnp.bfloat16), value2, preferred_element_type=jnp.float32)
        mixed = mixed + jnp.dot(e1.astype(jnp.bfloat16), v1_ref[:, lanes], preferred_element_type=jnp.float32)
        mixed = mixed + jnp.dot(
            e0.astype(jnp.bfloat16), v0_ref[:own_rows, lanes], preferred_element_type=jnp.float32
        )
        o_ref[:, lanes] = (mixed / total).astype(o_ref.dtype)

    def run(masked, own_rows):
        for head in range(q_ref.shape[1] // HD):
            one_head(slice(head * HD, (head + 1) * HD), masked, own_rows)

    early = first_row + count <= count

    @pl.when(early)
    def _():
        run(True, count)

    @pl.when(jnp.logical_not(early))
    def _():
        run(True, seg_rows)


def attend(seg_number, first_row, query_rows, keys, values, head_lo, head_count):
    count = query_rows.shape[0]
    seg_rows = keys[0].shape[0]
    step = 1
    width = step * HD
    q_spec = pl.BlockSpec((count, width), lambda h, scalars: (0, h + head_lo // step))
    kv_spec = pl.BlockSpec((seg_rows, width), lambda h, scalars: (0, h + head_lo // step))
    even_spec = pl.BlockSpec((seg_rows, width), lambda h, scalars: (0, (h + head_lo // step) * scalars[2]))
    odd_spec = pl.BlockSpec((seg_rows, width), lambda h, scalars: (0, (h + head_lo // step) * (1 - scalars[2])))
    o_spec = pl.BlockSpec((count, width), lambda h, scalars: (0, h))
    mem_specs = [even_spec, odd_spec, kv_spec, kv_spec]
    grid_spec = pltpu.PrefetchScalarGridSpec(
        num_scalar_prefetch=1,
        grid=(head_count // step,),
        in_specs=[q_spec] + mem_specs + mem_specs,
        out_specs=o_spec,
    )
    even = (seg_number % 2 == 0).astype(jnp.int32)
    scalars = jnp.stack([seg_number, first_row, even]).astype(jnp.int32)
    return pl.pallas_call(
        attention_kernel,
        grid_spec=grid_spec,
        out_shape=jax.ShapeDtypeStruct((count, head_count * HD), jnp.bfloat16),
        interpret=INTERPRET,
    )(scalars, query_rows, *keys, *values)


def body(hidden_states, queries, w_key, w_value):
    tok_rows = hidden_states.shape[0]
    width = w_key.shape[1]
    halves = lax.axis_size("fsdp")
    segs = lax.axis_size("seg")
    cols = width // halves
    piece = cols // 8
    half_number = lax.axis_index("fsdp")
    seg_number = lax.axis_index("seg")
    other_half = 1 - half_number
    first_is_mine = half_number == 0
    core = seg_number % 2
    is_key_core = core == 0

    def mine_of(array):
        return lax.dynamic_slice_in_dim(array, half_number * cols, cols, 1)

    def theirs_of(array):
        return lax.dynamic_slice_in_dim(array, other_half * cols, cols, 1)

    served = jnp.where(is_key_core, theirs_of(w_key), theirs_of(w_value))
    left_got = swap_halves(served[:, :piece])
    stride = segs // 8 if segs >= 16 else 0
    wrap_pairs = []
    for seg in range(segs):
        for half in range(halves):
            wrap_pairs.append(((seg ^ stride) * halves + (1 - half), seg * halves + half))
    right_got = lax.ppermute(served[:, piece:], ("seg", "fsdp"), wrap_pairs)
    piece_got = jnp.concatenate([left_got, right_got], axis=1)
    core_pairs = [(seg, seg ^ 1) for seg in range(segs)]
    piece_other = lax.ppermute(piece_got, "seg", core_pairs)
    key_got = jnp.where(is_key_core, piece_got, piece_other)
    value_got = jnp.where(is_key_core, piece_other, piece_got)

    hidden_got = swap_halves(hidden_states)

    key_weights = in_order(first_is_mine, mine_of(w_key), key_got, 0)
    value_weights = in_order(first_is_mine, mine_of(w_value), value_got, 0)
    hidden_rows = in_order(first_is_mine, hidden_states, hidden_got, 0)

    own_key = jnp.dot(hidden_rows, key_weights, preferred_element_type=jnp.float32).astype(jnp.bfloat16)
    own_value = jnp.dot(hidden_rows, value_weights, preferred_element_type=jnp.float32).astype(
        jnp.bfloat16
    )
    query_sent, own_key, own_value = lax.optimization_barrier((theirs_of(queries), own_key, own_value))
    query_got = swap_halves(query_sent)

    even_pairs = [(s, s + 2) for s in range(0, segs - 2, 2)]
    forward_pairs = [(s, s + 1) for s in range(0, segs - 1, 2)]

    def shifted(own):
        one = from_behind(own, "seg", 1)
        even_two = lax.ppermute(own, "seg", even_pairs)
        odd_two = lax.ppermute(one, "seg", forward_pairs)
        return (even_two, odd_two), one

    key_two, key_one = shifted(own_key)
    value_two, value_one = shifted(own_value)
    keys = (*key_two, key_one, own_key)
    values = (*value_two, value_one, own_value)

    heads = cols // HD
    lead = heads - heads // 4
    mine_q = mine_of(queries)
    mine_lead = attend(seg_number, half_number * tok_rows, mine_q, keys, values, 0, lead)
    query_got, mine_lead = lax.optimization_barrier((query_got, mine_lead))
    got = []
    for head_lo in range(0, heads, heads // 2):
        their_rows = attend(seg_number, other_half * tok_rows, query_got, keys, values, head_lo, heads // 2)
        got.append(swap_halves(their_rows))
    mine_q, their_rows = lax.optimization_barrier((mine_q, their_rows))
    mine_tail = attend(seg_number, half_number * tok_rows, mine_q, keys, values, lead, heads - lead)
    mine_rows = jnp.concatenate([mine_lead, mine_tail], axis=1)
    rows_got = jnp.concatenate(got, axis=1)
    return in_order(first_is_mine, mine_rows, rows_got, 1)


def solution(mesh):
    placed = (P(("seg", "fsdp"), None), P(("seg", "fsdp"), None), P("fsdp", None), P("fsdp", None))
    return jax.shard_map(
        body, mesh=mesh, in_specs=placed, out_specs=P(("seg", "fsdp"), None), check_vma=False
    )
```

```python
import functools

import jax
import jax.numpy as jnp
from jax import lax
from jax.experimental import pallas as pl
from jax.experimental.pallas import tpu as pltpu
from jax.sharding import PartitionSpec as P

HD = 128
MEM = 2
QBLOCK = 384
INTERPRET = False


def from_behind(value, axis, steps):
    count = lax.axis_size(axis)
    leading, last = (max(0, -steps), min(count, count - steps))
    return lax.ppermute(value, axis, [(source, source + steps) for source in range(leading, last)])


def swap_halves(value):
    return lax.ppermute(value, "fsdp", [(0, 1), (1, 0)])


def in_order(first_is_mine, mine, other, axis):
    lead = jnp.where(first_is_mine, mine, other)
    tail = jnp.where(first_is_mine, other, mine)
    return jnp.concatenate([lead, tail], axis=axis)


def attention_kernel(
    seg_ref, q_ref, k2e_ref, k2o_ref, k1_ref, k0_ref, v2e_ref, v2o_ref, v1_ref, v0_ref, o_ref
):
    seg = seg_ref[0]
    first_row = seg_ref[1]
    even = seg_ref[2]
    count = q_ref.shape[0]
    seg_rows = k0_ref.shape[0]
    dims = (((1,), (1,)), ((), ()))
    low = jnp.float32(-1e30)

    def one_head(lanes, masked, own_rows):
        query = q_ref[:, lanes]

        def scores_of(key):
            raw = lax.dot_general(query, key, dims, preferred_element_type=jnp.float32)
            return raw * HD ** (-0.5)

        open_rows = own_rows - count
        own_col = lax.broadcasted_iota(jnp.int32, (count, count), 1) + open_rows
        own_row = lax.broadcasted_iota(jnp.int32, (count, count), 0) + first_row
        causal = own_col <= own_row
        s0 = jnp.where(causal, scores_of(k0_ref[open_rows:own_rows, lanes]), low)
        s_open = scores_of(k0_ref[:open_rows, lanes]) if open_rows else None
        pick = lax.broadcasted_iota(jnp.int32, (seg_rows, HD), 0) < even * seg_rows
        s2 = scores_of(jnp.where(pick, k2e_ref[:, lanes], k2o_ref[:, lanes]))
        s1 = scores_of(k1_ref[:, lanes])
        if masked:
            col = lax.broadcasted_iota(jnp.int32, (count, seg_rows), 1)
            ok2 = col < jnp.where(seg >= 2, seg_rows, 0)
            ok1 = col < jnp.where(seg >= 1, seg_rows, 0)
            s2 = jnp.where(ok2, s2, low)
            s1 = jnp.where(ok1, s1, low)
        top = jnp.maximum(
            jnp.maximum(jnp.max(s2, axis=1, keepdims=True), jnp.max(s1, axis=1, keepdims=True)),
            jnp.max(s0, axis=1, keepdims=True),
        )
        if open_rows:
            top = jnp.maximum(top, jnp.max(s_open, axis=1, keepdims=True))
        e2 = jnp.exp(s2 - top)
        e1 = jnp.exp(s1 - top)
        if masked:
            e2 = jnp.where(ok2, e2, 0.0)
            e1 = jnp.where(ok1, e1, 0.0)
        e0 = jnp.where(causal, jnp.exp(s0 - top), 0.0)
        total = (
            jnp.sum(e2, axis=1, keepdims=True)
            + jnp.sum(e1, axis=1, keepdims=True)
            + jnp.sum(e0, axis=1, keepdims=True)
        )
        if open_rows:
            e_open = jnp.exp(s_open - top)
            total = total + jnp.sum(e_open, axis=1, keepdims=True)
        value2 = jnp.where(pick, v2e_ref[:, lanes], v2o_ref[:, lanes])
        mixed = jnp.dot(e2.astype(jnp.bfloat16), value2, preferred_element_type=jnp.float32)
        mixed = mixed + jnp.dot(e1.astype(jnp.bfloat16), v1_ref[:, lanes], preferred_element_type=jnp.float32)
        mixed = mixed + jnp.dot(
            e0.astype(jnp.bfloat16), v0_ref[open_rows:own_rows, lanes], preferred_element_type=jnp.float32
        )
        if open_rows:
            mixed = mixed + jnp.dot(
                e_open.astype(jnp.bfloat16), v0_ref[:open_rows, lanes], preferred_element_type=jnp.float32
            )
        o_ref[:, lanes] = (mixed / total).astype(o_ref.dtype)

    def run(masked, own_rows):
        for head in range(q_ref.shape[1] // HD):
            one_head(slice(head * HD, (head + 1) * HD), masked, own_rows)

    early = first_row + count <= count

    @pl.when(early)
    def _():
        run(True, count)

    @pl.when(jnp.logical_not(early))
    def _():
        run(True, seg_rows)


def attend(seg_number, first_row, query_rows, keys, values, head_lo, head_count):
    count = query_rows.shape[0]
    seg_rows = keys[0].shape[0]
    step = 1
    width = step * HD
    q_spec = pl.BlockSpec((count, width), lambda h, scalars: (0, h + head_lo // step))
    kv_spec = pl.BlockSpec((seg_rows, width), lambda h, scalars: (0, h + head_lo // step))
    even_spec = pl.BlockSpec((seg_rows, width), lambda h, scalars: (0, (h + head_lo // step) * scalars[2]))
    odd_spec = pl.BlockSpec((seg_rows, width), lambda h, scalars: (0, (h + head_lo // step) * (1 - scalars[2])))
    o_spec = pl.BlockSpec((count, width), lambda h, scalars: (0, h))
    mem_specs = [even_spec, odd_spec, kv_spec, kv_spec]
    grid_spec = pltpu.PrefetchScalarGridSpec(
        num_scalar_prefetch=1,
        grid=(head_count // step,),
        in_specs=[q_spec] + mem_specs + mem_specs,
        out_specs=o_spec,
    )
    even = (seg_number % 2 == 0).astype(jnp.int32)
    scalars = jnp.stack([seg_number, first_row, even]).astype(jnp.int32)
    return pl.pallas_call(
        attention_kernel,
        grid_spec=grid_spec,
        out_shape=jax.ShapeDtypeStruct((count, head_count * HD), jnp.bfloat16),
        interpret=INTERPRET,
    )(scalars, query_rows, *keys, *values)


def body(hidden_states, queries, w_key, w_value):
    tok_rows = hidden_states.shape[0]
    width = w_key.shape[1]
    halves = lax.axis_size("fsdp")
    segs = lax.axis_size("seg")
    cols = width // halves
    piece = cols // 8
    half_number = lax.axis_index("fsdp")
    seg_number = lax.axis_index("seg")
    other_half = 1 - half_number
    first_is_mine = half_number == 0
    core = seg_number % 2
    is_key_core = core == 0

    def mine_of(array):
        return lax.dynamic_slice_in_dim(array, half_number * cols, cols, 1)

    def theirs_of(array):
        return lax.dynamic_slice_in_dim(array, other_half * cols, cols, 1)

    served = jnp.where(is_key_core, theirs_of(w_key), theirs_of(w_value))
    left_got = swap_halves(served[:, :piece])
    stride = segs // 8 if segs >= 16 else 0
    wrap_pairs = []
    for seg in range(segs):
        for half in range(halves):
            wrap_pairs.append(((seg ^ stride) * halves + (1 - half), seg * halves + half))
    right_got = lax.ppermute(served[:, piece:], ("seg", "fsdp"), wrap_pairs)
    piece_got = jnp.concatenate([left_got, right_got], axis=1)
    core_pairs = [(seg, seg ^ 1) for seg in range(segs)]
    piece_other = lax.ppermute(piece_got, "seg", core_pairs)
    key_got = jnp.where(is_key_core, piece_got, piece_other)
    value_got = jnp.where(is_key_core, piece_other, piece_got)

    hidden_got = swap_halves(hidden_states)

    key_weights = in_order(first_is_mine, mine_of(w_key), key_got, 0)
    value_weights = in_order(first_is_mine, mine_of(w_value), value_got, 0)
    hidden_rows = in_order(first_is_mine, hidden_states, hidden_got, 0)

    own_key = jnp.dot(hidden_rows, key_weights, preferred_element_type=jnp.float32).astype(jnp.bfloat16)
    own_value = jnp.dot(hidden_rows, value_weights, preferred_element_type=jnp.float32).astype(
        jnp.bfloat16
    )
    query_sent, own_key, own_value = lax.optimization_barrier((theirs_of(queries), own_key, own_value))
    query_got = swap_halves(query_sent)

    even_pairs = [(s, s + 2) for s in range(0, segs - 2, 2)]
    forward_pairs = [(s, s + 1) for s in range(0, segs - 1, 2)]

    def shifted(own):
        one = from_behind(own, "seg", 1)
        even_two = lax.ppermute(own, "seg", even_pairs)
        odd_two = lax.ppermute(one, "seg", forward_pairs)
        return (even_two, odd_two), one

    key_two, key_one = shifted(own_key)
    value_two, value_one = shifted(own_value)
    keys = (*key_two, key_one, own_key)
    values = (*value_two, value_one, own_value)

    heads = cols // HD
    lead = heads - heads // 4
    mine_q = mine_of(queries)
    mine_lead = attend(seg_number, half_number * tok_rows, mine_q, keys, values, 0, lead)
    query_got, mine_lead = lax.optimization_barrier((query_got, mine_lead))
    got = []
    for head_lo in range(0, heads, heads // 2):
        their_rows = attend(seg_number, other_half * tok_rows, query_got, keys, values, head_lo, heads // 2)
        got.append(swap_halves(their_rows))
    mine_q, their_rows = lax.optimization_barrier((mine_q, their_rows))
    mine_tail = attend(seg_number, half_number * tok_rows, mine_q, keys, values, lead, heads - lead)
    mine_rows = jnp.concatenate([mine_lead, mine_tail], axis=1)
    rows_got = jnp.concatenate(got, axis=1)
    return in_order(first_is_mine, mine_rows, rows_got, 1)


def solution(mesh):
    placed = (P(("seg", "fsdp"), None), P(("seg", "fsdp"), None), P("fsdp", None), P("fsdp", None))
    return jax.shard_map(
        body, mesh=mesh, in_specs=placed, out_specs=P(("seg", "fsdp"), None), check_vma=False
    )
```

```python
import functools

import jax
import jax.numpy as jnp
from jax import lax
from jax.experimental import pallas as pl
from jax.experimental.pallas import tpu as pltpu
from jax.sharding import PartitionSpec as P

HD = 128
MEM = 2
QBLOCK = 384
INTERPRET = False


def from_behind(value, axis, steps):
    count = lax.axis_size(axis)
    leading, last = (max(0, -steps), min(count, count - steps))
    return lax.ppermute(value, axis, [(source, source + steps) for source in range(leading, last)])


def swap_halves(value):
    return lax.ppermute(value, "fsdp", [(0, 1), (1, 0)])


def in_order(first_is_mine, mine, other, axis):
    lead = jnp.where(first_is_mine, mine, other)
    tail = jnp.where(first_is_mine, other, mine)
    return jnp.concatenate([lead, tail], axis=axis)


def attention_kernel(
    seg_ref, q_ref, k2e_ref, k2o_ref, k1_ref, k0_ref, v2e_ref, v2o_ref, v1_ref, v0_ref, o_ref
):
    seg = seg_ref[0]
    first_row = seg_ref[1]
    even = seg_ref[2]
    count = q_ref.shape[0]
    seg_rows = k0_ref.shape[0]
    dims = (((1,), (1,)), ((), ()))
    low = jnp.float32(-1e30)

    def one_head(lanes, masked, own_rows):
        query = q_ref[:, lanes]

        def scores_of(key):
            raw = lax.dot_general(query, key, dims, preferred_element_type=jnp.float32)
            return raw * HD ** (-0.5)

        open_rows = own_rows - count
        own_col = lax.broadcasted_iota(jnp.int32, (count, count), 1) + open_rows
        own_row = lax.broadcasted_iota(jnp.int32, (count, count), 0) + first_row
        causal = own_col <= own_row
        s0 = jnp.where(causal, scores_of(k0_ref[open_rows:own_rows, lanes]), low)
        s_open = scores_of(k0_ref[:open_rows, lanes]) if open_rows else None
        pick = lax.broadcasted_iota(jnp.int32, (seg_rows, HD), 0) < even * seg_rows
        s2 = scores_of(jnp.where(pick, k2e_ref[:, lanes], k2o_ref[:, lanes]))
        s1 = scores_of(k1_ref[:, lanes])
        if masked:
            col = lax.broadcasted_iota(jnp.int32, (count, seg_rows), 1)
            ok2 = col < jnp.where(seg >= 2, seg_rows, 0)
            ok1 = col < jnp.where(seg >= 1, seg_rows, 0)
            s2 = jnp.where(ok2, s2, low)
            s1 = jnp.where(ok1, s1, low)
        top = jnp.maximum(
            jnp.maximum(jnp.max(s2, axis=1, keepdims=True), jnp.max(s1, axis=1, keepdims=True)),
            jnp.max(s0, axis=1, keepdims=True),
        )
        if open_rows:
            top = jnp.maximum(top, jnp.max(s_open, axis=1, keepdims=True))
        e2 = jnp.exp(s2 - top)
        e1 = jnp.exp(s1 - top)
        if masked:
            e2 = jnp.where(ok2, e2, 0.0)
            e1 = jnp.where(ok1, e1, 0.0)
        e0 = jnp.where(causal, jnp.exp(s0 - top), 0.0)
        total = (
            jnp.sum(e2, axis=1, keepdims=True)
            + jnp.sum(e1, axis=1, keepdims=True)
            + jnp.sum(e0, axis=1, keepdims=True)
        )
        if open_rows:
            e_open = jnp.exp(s_open - top)
            total = total + jnp.sum(e_open, axis=1, keepdims=True)
        value2 = jnp.where(pick, v2e_ref[:, lanes], v2o_ref[:, lanes])
        mixed = jnp.dot(e2.astype(jnp.bfloat16), value2, preferred_element_type=jnp.float32)
        mixed = mixed + jnp.dot(e1.astype(jnp.bfloat16), v1_ref[:, lanes], preferred_element_type=jnp.float32)
        mixed = mixed + jnp.dot(
            e0.astype(jnp.bfloat16), v0_ref[open_rows:own_rows, lanes], preferred_element_type=jnp.float32
        )
        if open_rows:
            mixed = mixed + jnp.dot(
                e_open.astype(jnp.bfloat16), v0_ref[:open_rows, lanes], preferred_element_type=jnp.float32
            )
        o_ref[:, lanes] = (mixed / total).astype(o_ref.dtype)

    def run(masked, own_rows):
        for head in range(q_ref.shape[1] // HD):
            one_head(slice(head * HD, (head + 1) * HD), masked, own_rows)

    early = first_row + count <= count

    @pl.when(early)
    def _():
        run(True, count)

    @pl.when(jnp.logical_not(early))
    def _():
        run(True, seg_rows)


def attend(seg_number, first_row, query_rows, keys, values, head_lo, head_count):
    count = query_rows.shape[0]
    seg_rows = keys[0].shape[0]
    step = 1
    width = step * HD
    q_spec = pl.BlockSpec((count, width), lambda h, scalars: (0, h + head_lo // step))
    kv_spec = pl.BlockSpec((seg_rows, width), lambda h, scalars: (0, h + head_lo // step))
    even_spec = pl.BlockSpec((seg_rows, width), lambda h, scalars: (0, (h + head_lo // step) * scalars[2]))
    odd_spec = pl.BlockSpec((seg_rows, width), lambda h, scalars: (0, (h + head_lo // step) * (1 - scalars[2])))
    o_spec = pl.BlockSpec((count, width), lambda h, scalars: (0, h))
    mem_specs = [even_spec, odd_spec, kv_spec, kv_spec]
    grid_spec = pltpu.PrefetchScalarGridSpec(
        num_scalar_prefetch=1,
        grid=(head_count // step,),
        in_specs=[q_spec] + mem_specs + mem_specs,
        out_specs=o_spec,
    )
    even = (seg_number % 2 == 0).astype(jnp.int32)
    scalars = jnp.stack([seg_number, first_row, even]).astype(jnp.int32)
    return pl.pallas_call(
        attention_kernel,
        grid_spec=grid_spec,
        out_shape=jax.ShapeDtypeStruct((count, head_count * HD), jnp.bfloat16),
        interpret=INTERPRET,
    )(scalars, query_rows, *keys, *values)


def body(hidden_states, queries, w_key, w_value):
    tok_rows = hidden_states.shape[0]
    width = w_key.shape[1]
    halves = lax.axis_size("fsdp")
    segs = lax.axis_size("seg")
    cols = width // halves
    piece = cols // 8
    half_number = lax.axis_index("fsdp")
    seg_number = lax.axis_index("seg")
    other_half = 1 - half_number
    first_is_mine = half_number == 0
    core = seg_number % 2
    is_key_core = core == 0

    def mine_of(array):
        return lax.dynamic_slice_in_dim(array, half_number * cols, cols, 1)

    def theirs_of(array):
        return lax.dynamic_slice_in_dim(array, other_half * cols, cols, 1)

    served = jnp.where(is_key_core, theirs_of(w_key), theirs_of(w_value))
    left_got = swap_halves(served[:, :piece])
    stride = segs // 8 if segs >= 16 else 0
    wrap_pairs = []
    for seg in range(segs):
        for half in range(halves):
            wrap_pairs.append(((seg ^ stride) * halves + (1 - half), seg * halves + half))
    right_got = lax.ppermute(served[:, piece:], ("seg", "fsdp"), wrap_pairs)
    piece_got = jnp.concatenate([left_got, right_got], axis=1)
    core_pairs = [(seg, seg ^ 1) for seg in range(segs)]
    piece_other = lax.ppermute(piece_got, "seg", core_pairs)
    key_got = jnp.where(is_key_core, piece_got, piece_other)
    value_got = jnp.where(is_key_core, piece_other, piece_got)

    hidden_got = swap_halves(hidden_states)

    key_weights = in_order(first_is_mine, mine_of(w_key), key_got, 0)
    value_weights = in_order(first_is_mine, mine_of(w_value), value_got, 0)
    hidden_rows = in_order(first_is_mine, hidden_states, hidden_got, 0)

    own_key = jnp.dot(hidden_rows, key_weights, preferred_element_type=jnp.float32).astype(jnp.bfloat16)
    own_value = jnp.dot(hidden_rows, value_weights, preferred_element_type=jnp.float32).astype(
        jnp.bfloat16
    )
    query_sent, own_key, own_value = lax.optimization_barrier((theirs_of(queries), own_key, own_value))
    query_got = swap_halves(query_sent)

    even_pairs = [(s, s + 2) for s in range(0, segs - 2, 2)]
    forward_pairs = [(s, s + 1) for s in range(0, segs - 1, 2)]

    def shifted(own):
        one = from_behind(own, "seg", 1)
        even_two = lax.ppermute(own, "seg", even_pairs)
        odd_two = lax.ppermute(one, "seg", forward_pairs)
        return (even_two, odd_two), one

    key_two, key_one = shifted(own_key)
    value_two, value_one = shifted(own_value)
    keys = (*key_two, key_one, own_key)
    values = (*value_two, value_one, own_value)

    heads = cols // HD
    lead = heads - 3 * heads // 8
    mine_q = mine_of(queries)
    mine_lead = attend(seg_number, half_number * tok_rows, mine_q, keys, values, 0, lead)
    query_got, mine_lead = lax.optimization_barrier((query_got, mine_lead))
    got = []
    for head_lo in range(0, heads, heads // 2):
        their_rows = attend(seg_number, other_half * tok_rows, query_got, keys, values, head_lo, heads // 2)
        got.append(swap_halves(their_rows))
    mine_q, their_rows = lax.optimization_barrier((mine_q, their_rows))
    mine_tail = attend(seg_number, half_number * tok_rows, mine_q, keys, values, lead, heads - lead)
    mine_first = jnp.concatenate([mine_lead, mine_tail, *got], axis=1)
    theirs_first = jnp.concatenate([*got, mine_lead, mine_tail], axis=1)
    return jnp.where(first_is_mine, mine_first, theirs_first)


def solution(mesh):
    placed = (P(("seg", "fsdp"), None), P(("seg", "fsdp"), None), P("fsdp", None), P("fsdp", None))
    return jax.shard_map(
        body, mesh=mesh, in_specs=placed, out_specs=P(("seg", "fsdp"), None), check_vma=False
    )
```

```python
import functools

import jax
import jax.numpy as jnp
from jax import lax
from jax.experimental import pallas as pl
from jax.experimental.pallas import tpu as pltpu
from jax.sharding import PartitionSpec as P

HD = 128
MEM = 2
QBLOCK = 384
INTERPRET = False


def from_behind(value, axis, steps):
    count = lax.axis_size(axis)
    leading, last = (max(0, -steps), min(count, count - steps))
    return lax.ppermute(value, axis, [(source, source + steps) for source in range(leading, last)])


def swap_halves(value):
    return lax.ppermute(value, "fsdp", [(0, 1), (1, 0)])


def in_order(first_is_mine, mine, other, axis):
    lead = jnp.where(first_is_mine, mine, other)
    tail = jnp.where(first_is_mine, other, mine)
    return jnp.concatenate([lead, tail], axis=axis)


def attention_kernel(
    seg_ref, q_ref, k2e_ref, k2o_ref, k1_ref, k0_ref, v2e_ref, v2o_ref, v1_ref, v0_ref, o_ref
):
    seg = seg_ref[0]
    first_row = seg_ref[1]
    even = seg_ref[2]
    count = q_ref.shape[0]
    seg_rows = k0_ref.shape[0]
    dims = (((1,), (1,)), ((), ()))
    low = jnp.float32(-1e30)

    def one_head(lanes, masked, own_rows):
        query = q_ref[:, lanes]

        def scores_of(key):
            raw = lax.dot_general(query, key, dims, preferred_element_type=jnp.float32)
            return raw * HD ** (-0.5)

        open_rows = own_rows - count
        own_col = lax.broadcasted_iota(jnp.int32, (count, count), 1) + open_rows
        own_row = lax.broadcasted_iota(jnp.int32, (count, count), 0) + first_row
        causal = own_col <= own_row
        s0 = jnp.where(causal, scores_of(k0_ref[open_rows:own_rows, lanes]), low)
        s_open = scores_of(k0_ref[:open_rows, lanes]) if open_rows else None
        pick = lax.broadcasted_iota(jnp.int32, (seg_rows, HD), 0) < even * seg_rows
        s2 = scores_of(jnp.where(pick, k2e_ref[:, lanes], k2o_ref[:, lanes]))
        s1 = scores_of(k1_ref[:, lanes])
        if masked:
            col = lax.broadcasted_iota(jnp.int32, (count, seg_rows), 1)
            ok2 = col < jnp.where(seg >= 2, seg_rows, 0)
            ok1 = col < jnp.where(seg >= 1, seg_rows, 0)
            s2 = jnp.where(ok2, s2, low)
            s1 = jnp.where(ok1, s1, low)
        top = jnp.maximum(
            jnp.maximum(jnp.max(s2, axis=1, keepdims=True), jnp.max(s1, axis=1, keepdims=True)),
            jnp.max(s0, axis=1, keepdims=True),
        )
        if open_rows:
            top = jnp.maximum(top, jnp.max(s_open, axis=1, keepdims=True))
        e2 = jnp.exp(s2 - top)
        e1 = jnp.exp(s1 - top)
        if masked:
            e2 = jnp.where(ok2, e2, 0.0)
            e1 = jnp.where(ok1, e1, 0.0)
        e0 = jnp.where(causal, jnp.exp(s0 - top), 0.0)
        total = (
            jnp.sum(e2, axis=1, keepdims=True)
            + jnp.sum(e1, axis=1, keepdims=True)
            + jnp.sum(e0, axis=1, keepdims=True)
        )
        if open_rows:
            e_open = jnp.exp(s_open - top)
            total = total + jnp.sum(e_open, axis=1, keepdims=True)
        value2 = jnp.where(pick, v2e_ref[:, lanes], v2o_ref[:, lanes])
        mixed = jnp.dot(e2.astype(jnp.bfloat16), value2, preferred_element_type=jnp.float32)
        mixed = mixed + jnp.dot(e1.astype(jnp.bfloat16), v1_ref[:, lanes], preferred_element_type=jnp.float32)
        mixed = mixed + jnp.dot(
            e0.astype(jnp.bfloat16), v0_ref[open_rows:own_rows, lanes], preferred_element_type=jnp.float32
        )
        if open_rows:
            mixed = mixed + jnp.dot(
                e_open.astype(jnp.bfloat16), v0_ref[:open_rows, lanes], preferred_element_type=jnp.float32
            )
        o_ref[:, lanes] = (mixed / total).astype(o_ref.dtype)

    def run(masked, own_rows):
        for head in range(q_ref.shape[1] // HD):
            one_head(slice(head * HD, (head + 1) * HD), masked, own_rows)

    early = first_row + count <= count

    @pl.when(early)
    def _():
        run(True, count)

    @pl.when(jnp.logical_not(early))
    def _():
        run(True, seg_rows)


def attend(seg_number, first_row, query_rows, keys, values, head_lo, head_count):
    count = query_rows.shape[0]
    seg_rows = keys[0].shape[0]
    step = 1
    width = step * HD
    q_spec = pl.BlockSpec((count, width), lambda h, scalars: (0, h + head_lo // step))
    kv_spec = pl.BlockSpec((seg_rows, width), lambda h, scalars: (0, h + head_lo // step))
    even_spec = pl.BlockSpec((seg_rows, width), lambda h, scalars: (0, (h + head_lo // step) * scalars[2]))
    odd_spec = pl.BlockSpec((seg_rows, width), lambda h, scalars: (0, (h + head_lo // step) * (1 - scalars[2])))
    o_spec = pl.BlockSpec((count, width), lambda h, scalars: (0, h))
    mem_specs = [even_spec, odd_spec, kv_spec, kv_spec]
    grid_spec = pltpu.PrefetchScalarGridSpec(
        num_scalar_prefetch=1,
        grid=(head_count // step,),
        in_specs=[q_spec] + mem_specs + mem_specs,
        out_specs=o_spec,
    )
    even = (seg_number % 2 == 0).astype(jnp.int32)
    scalars = jnp.stack([seg_number, first_row, even]).astype(jnp.int32)
    return pl.pallas_call(
        attention_kernel,
        grid_spec=grid_spec,
        out_shape=jax.ShapeDtypeStruct((count, head_count * HD), jnp.bfloat16),
        interpret=INTERPRET,
    )(scalars, query_rows, *keys, *values)


def body(hidden_states, queries, w_key, w_value):
    tok_rows = hidden_states.shape[0]
    width = w_key.shape[1]
    halves = lax.axis_size("fsdp")
    segs = lax.axis_size("seg")
    cols = width // halves
    piece = cols // 8
    half_number = lax.axis_index("fsdp")
    seg_number = lax.axis_index("seg")
    other_half = 1 - half_number
    first_is_mine = half_number == 0
    core = seg_number % 2
    is_key_core = core == 0

    def mine_of(array):
        return lax.dynamic_slice_in_dim(array, half_number * cols, cols, 1)

    def theirs_of(array):
        return lax.dynamic_slice_in_dim(array, other_half * cols, cols, 1)

    served = jnp.where(is_key_core, theirs_of(w_key), theirs_of(w_value))
    left_got = swap_halves(served[:, :piece])
    stride = segs // 8 if segs >= 16 else 0
    wrap_pairs = []
    for seg in range(segs):
        for half in range(halves):
            wrap_pairs.append(((seg ^ stride) * halves + (1 - half), seg * halves + half))
    right_got = lax.ppermute(served[:, piece:], ("seg", "fsdp"), wrap_pairs)
    piece_got = jnp.concatenate([left_got, right_got], axis=1)
    core_pairs = [(seg, seg ^ 1) for seg in range(segs)]
    piece_other = lax.ppermute(piece_got, "seg", core_pairs)
    key_got = jnp.where(is_key_core, piece_got, piece_other)
    value_got = jnp.where(is_key_core, piece_other, piece_got)

    hidden_got = swap_halves(hidden_states)

    key_weights = in_order(first_is_mine, mine_of(w_key), key_got, 0)
    value_weights = in_order(first_is_mine, mine_of(w_value), value_got, 0)
    hidden_rows = in_order(first_is_mine, hidden_states, hidden_got, 0)

    own_key = jnp.dot(hidden_rows, key_weights, preferred_element_type=jnp.float32).astype(jnp.bfloat16)
    own_value = jnp.dot(hidden_rows, value_weights, preferred_element_type=jnp.float32).astype(
        jnp.bfloat16
    )
    query_sent, own_key, own_value = lax.optimization_barrier((theirs_of(queries), own_key, own_value))
    query_got = swap_halves(query_sent)

    even_pairs = [(s, s + 2) for s in range(0, segs - 2, 2)]
    forward_pairs = [(s, s + 1) for s in range(0, segs - 1, 2)]

    def shifted(own):
        one = from_behind(own, "seg", 1)
        even_two = lax.ppermute(own, "seg", even_pairs)
        odd_two = lax.ppermute(one, "seg", forward_pairs)
        return (even_two, odd_two), one

    key_two, key_one = shifted(own_key)
    value_two, value_one = shifted(own_value)
    keys = (*key_two, key_one, own_key)
    values = (*value_two, value_one, own_value)

    heads = cols // HD
    lead = heads - heads // 4
    mine_q = mine_of(queries)
    mine_lead = attend(seg_number, half_number * tok_rows, mine_q, keys, values, 0, lead)
    query_got, mine_lead = lax.optimization_barrier((query_got, mine_lead))
    got = []
    split = heads - 3 * heads // 8
    for head_lo, head_count in ((0, split), (split, heads - split)):
        their_rows = attend(seg_number, other_half * tok_rows, query_got, keys, values, head_lo, head_count)
        got.append(swap_halves(their_rows))
    mine_q, their_rows = lax.optimization_barrier((mine_q, their_rows))
    mine_tail = attend(seg_number, half_number * tok_rows, mine_q, keys, values, lead, heads - lead)
    mine_first = jnp.concatenate([mine_lead, mine_tail, *got], axis=1)
    theirs_first = jnp.concatenate([*got, mine_lead, mine_tail], axis=1)
    return jnp.where(first_is_mine, mine_first, theirs_first)


def solution(mesh):
    placed = (P(("seg", "fsdp"), None), P(("seg", "fsdp"), None), P("fsdp", None), P("fsdp", None))
    return jax.shard_map(
        body, mesh=mesh, in_specs=placed, out_specs=P(("seg", "fsdp"), None), check_vma=False
    )
```

```python
import functools

import jax
import jax.numpy as jnp
from jax import lax
from jax.experimental import pallas as pl
from jax.experimental.pallas import tpu as pltpu
from jax.sharding import PartitionSpec as P

HD = 128
MEM = 2
QBLOCK = 384
INTERPRET = False


def from_behind(value, axis, steps):
    count = lax.axis_size(axis)
    leading, last = (max(0, -steps), min(count, count - steps))
    return lax.ppermute(value, axis, [(source, source + steps) for source in range(leading, last)])


def swap_halves(value):
    return lax.ppermute(value, "fsdp", [(0, 1), (1, 0)])


def in_order(first_is_mine, mine, other, axis):
    lead = jnp.where(first_is_mine, mine, other)
    tail = jnp.where(first_is_mine, other, mine)
    return jnp.concatenate([lead, tail], axis=axis)


def attention_kernel(
    seg_ref, q_ref, k2e_ref, k2o_ref, k1_ref, k0_ref, v2e_ref, v2o_ref, v1_ref, v0_ref, o_ref
):
    seg = seg_ref[0]
    first_row = seg_ref[1]
    even = seg_ref[2]
    count = q_ref.shape[0]
    seg_rows = k0_ref.shape[0]
    dims = (((1,), (1,)), ((), ()))
    low = jnp.float32(-1e30)

    def one_head(lanes, masked, own_rows):
        query = q_ref[:, lanes]

        def scores_of(key):
            raw = lax.dot_general(query, key, dims, preferred_element_type=jnp.float32)
            return raw * HD ** (-0.5)

        open_rows = own_rows - count
        own_col = lax.broadcasted_iota(jnp.int32, (count, count), 1) + open_rows
        own_row = lax.broadcasted_iota(jnp.int32, (count, count), 0) + first_row
        causal = own_col <= own_row
        s0 = jnp.where(causal, scores_of(k0_ref[open_rows:own_rows, lanes]), low)
        s_open = scores_of(k0_ref[:open_rows, lanes]) if open_rows else None
        pick = lax.broadcasted_iota(jnp.int32, (seg_rows, HD), 0) < even * seg_rows
        s2 = scores_of(jnp.where(pick, k2e_ref[:, lanes], k2o_ref[:, lanes]))
        s1 = scores_of(k1_ref[:, lanes])
        if masked:
            col = lax.broadcasted_iota(jnp.int32, (count, seg_rows), 1)
            ok2 = col < jnp.where(seg >= 2, seg_rows, 0)
            ok1 = col < jnp.where(seg >= 1, seg_rows, 0)
            s2 = jnp.where(ok2, s2, low)
            s1 = jnp.where(ok1, s1, low)
        top = jnp.maximum(
            jnp.maximum(jnp.max(s2, axis=1, keepdims=True), jnp.max(s1, axis=1, keepdims=True)),
            jnp.max(s0, axis=1, keepdims=True),
        )
        if open_rows:
            top = jnp.maximum(top, jnp.max(s_open, axis=1, keepdims=True))
        e2 = jnp.exp(s2 - top)
        e1 = jnp.exp(s1 - top)
        if masked:
            e2 = jnp.where(ok2, e2, 0.0)
            e1 = jnp.where(ok1, e1, 0.0)
        e0 = jnp.where(causal, jnp.exp(s0 - top), 0.0)
        total = (
            jnp.sum(e2, axis=1, keepdims=True)
            + jnp.sum(e1, axis=1, keepdims=True)
            + jnp.sum(e0, axis=1, keepdims=True)
        )
        if open_rows:
            e_open = jnp.exp(s_open - top)
            total = total + jnp.sum(e_open, axis=1, keepdims=True)
        value2 = jnp.where(pick, v2e_ref[:, lanes], v2o_ref[:, lanes])
        mixed = jnp.dot(e2.astype(jnp.bfloat16), value2, preferred_element_type=jnp.float32)
        mixed = mixed + jnp.dot(e1.astype(jnp.bfloat16), v1_ref[:, lanes], preferred_element_type=jnp.float32)
        mixed = mixed + jnp.dot(
            e0.astype(jnp.bfloat16), v0_ref[open_rows:own_rows, lanes], preferred_element_type=jnp.float32
        )
        if open_rows:
            mixed = mixed + jnp.dot(
                e_open.astype(jnp.bfloat16), v0_ref[:open_rows, lanes], preferred_element_type=jnp.float32
            )
        o_ref[:, lanes] = (mixed / total).astype(o_ref.dtype)

    def run(masked, own_rows):
        for head in range(q_ref.shape[1] // HD):
            one_head(slice(head * HD, (head + 1) * HD), masked, own_rows)

    early = first_row + count <= count

    @pl.when(early)
    def _():
        run(True, count)

    @pl.when(jnp.logical_not(early))
    def _():
        run(True, seg_rows)


def attend(seg_number, first_row, query_rows, keys, values, head_lo, head_count):
    count = query_rows.shape[0]
    seg_rows = keys[0].shape[0]
    step = 1
    width = step * HD
    q_spec = pl.BlockSpec((count, width), lambda h, scalars: (0, h + head_lo // step))
    kv_spec = pl.BlockSpec((seg_rows, width), lambda h, scalars: (0, h + head_lo // step))
    even_spec = pl.BlockSpec((seg_rows, width), lambda h, scalars: (0, (h + head_lo // step) * scalars[2]))
    odd_spec = pl.BlockSpec((seg_rows, width), lambda h, scalars: (0, (h + head_lo // step) * (1 - scalars[2])))
    o_spec = pl.BlockSpec((count, width), lambda h, scalars: (0, h))
    mem_specs = [even_spec, odd_spec, kv_spec, kv_spec]
    grid_spec = pltpu.PrefetchScalarGridSpec(
        num_scalar_prefetch=1,
        grid=(head_count // step,),
        in_specs=[q_spec] + mem_specs + mem_specs,
        out_specs=o_spec,
    )
    even = (seg_number % 2 == 0).astype(jnp.int32)
    scalars = jnp.stack([seg_number, first_row, even]).astype(jnp.int32)
    return pl.pallas_call(
        attention_kernel,
        grid_spec=grid_spec,
        out_shape=jax.ShapeDtypeStruct((count, head_count * HD), jnp.bfloat16),
        interpret=INTERPRET,
    )(scalars, query_rows, *keys, *values)


def body(hidden_states, queries, w_key, w_value):
    tok_rows = hidden_states.shape[0]
    width = w_key.shape[1]
    halves = lax.axis_size("fsdp")
    segs = lax.axis_size("seg")
    cols = width // halves
    piece = cols // 8
    half_number = lax.axis_index("fsdp")
    seg_number = lax.axis_index("seg")
    other_half = 1 - half_number
    first_is_mine = half_number == 0
    core = seg_number % 2
    is_key_core = core == 0

    def mine_of(array):
        return lax.dynamic_slice_in_dim(array, half_number * cols, cols, 1)

    def theirs_of(array):
        return lax.dynamic_slice_in_dim(array, other_half * cols, cols, 1)

    served = jnp.where(is_key_core, theirs_of(w_key), theirs_of(w_value))
    left_got = swap_halves(served[:, :piece])
    stride = segs // 8 if segs >= 16 else 0
    wrap_pairs = []
    for seg in range(segs):
        for half in range(halves):
            wrap_pairs.append(((seg ^ stride) * halves + (1 - half), seg * halves + half))
    right_got = lax.ppermute(served[:, piece:], ("seg", "fsdp"), wrap_pairs)
    piece_got = jnp.concatenate([left_got, right_got], axis=1)
    core_pairs = [(seg, seg ^ 1) for seg in range(segs)]
    piece_other = lax.ppermute(piece_got, "seg", core_pairs)
    key_got = jnp.where(is_key_core, piece_got, piece_other)
    value_got = jnp.where(is_key_core, piece_other, piece_got)

    hidden_got = swap_halves(hidden_states)

    hidden_rows = in_order(first_is_mine, hidden_states, hidden_got, 0)
    channels = w_key.shape[0]
    hidden_rows = jnp.where(first_is_mine, hidden_rows, jnp.roll(hidden_rows, -channels, axis=1))

    def project(local, got):
        own = jnp.dot(hidden_rows[:, :channels], mine_of(local), preferred_element_type=jnp.float32)
        own = own + jnp.dot(hidden_rows[:, channels:], got, preferred_element_type=jnp.float32)
        return own.astype(jnp.bfloat16)

    own_key = project(w_key, key_got)
    own_value = project(w_value, value_got)
    query_sent, own_key, own_value = lax.optimization_barrier((theirs_of(queries), own_key, own_value))
    query_got = swap_halves(query_sent)

    even_pairs = [(s, s + 2) for s in range(0, segs - 2, 2)]
    forward_pairs = [(s, s + 1) for s in range(0, segs - 1, 2)]

    def shifted(own):
        one = from_behind(own, "seg", 1)
        even_two = lax.ppermute(own, "seg", even_pairs)
        odd_two = lax.ppermute(one, "seg", forward_pairs)
        return (even_two, odd_two), one

    key_two, key_one = shifted(own_key)
    value_two, value_one = shifted(own_value)
    keys = (*key_two, key_one, own_key)
    values = (*value_two, value_one, own_value)

    heads = cols // HD
    lead = heads - heads // 4
    mine_q = mine_of(queries)
    mine_lead = attend(seg_number, half_number * tok_rows, mine_q, keys, values, 0, lead)
    query_got, mine_lead = lax.optimization_barrier((query_got, mine_lead))
    got = []
    split = heads - 3 * heads // 8
    for head_lo, head_count in ((0, split), (split, heads - split)):
        their_rows = attend(seg_number, other_half * tok_rows, query_got, keys, values, head_lo, head_count)
        got.append(swap_halves(their_rows))
    mine_q, their_rows = lax.optimization_barrier((mine_q, their_rows))
    mine_tail = attend(seg_number, half_number * tok_rows, mine_q, keys, values, lead, heads - lead)
    mine_first = jnp.concatenate([mine_lead, mine_tail, *got], axis=1)
    theirs_first = jnp.concatenate([*got, mine_lead, mine_tail], axis=1)
    return jnp.where(first_is_mine, mine_first, theirs_first)


def solution(mesh):
    placed = (P(("seg", "fsdp"), None), P(("seg", "fsdp"), None), P("fsdp", None), P("fsdp", None))
    return jax.shard_map(
        body, mesh=mesh, in_specs=placed, out_specs=P(("seg", "fsdp"), None), check_vma=False
    )
```

```python
import functools

import jax
import jax.numpy as jnp
from jax import lax
from jax.experimental import pallas as pl
from jax.experimental.pallas import tpu as pltpu
from jax.sharding import PartitionSpec as P

HD = 128
MEM = 2
QBLOCK = 384
INTERPRET = False


def from_behind(value, axis, steps):
    count = lax.axis_size(axis)
    leading, last = (max(0, -steps), min(count, count - steps))
    return lax.ppermute(value, axis, [(source, source + steps) for source in range(leading, last)])


def swap_halves(value):
    return lax.ppermute(value, "fsdp", [(0, 1), (1, 0)])


def in_order(first_is_mine, mine, other, axis):
    lead = jnp.where(first_is_mine, mine, other)
    tail = jnp.where(first_is_mine, other, mine)
    return jnp.concatenate([lead, tail], axis=axis)


def attention_kernel(
    seg_ref, q_ref, k2e_ref, k2o_ref, k1_ref, k0_ref, v2e_ref, v2o_ref, v1_ref, v0_ref, o_ref
):
    seg = seg_ref[0]
    first_row = seg_ref[1]
    even = seg_ref[2]
    count = q_ref.shape[0]
    seg_rows = k0_ref.shape[0]
    dims = (((1,), (1,)), ((), ()))
    low = jnp.float32(-1e30)

    def one_head(lanes, masked, own_rows):
        query = q_ref[:, lanes]

        def scores_of(key):
            raw = lax.dot_general(query, key, dims, preferred_element_type=jnp.float32)
            return raw * HD ** (-0.5)

        open_rows = own_rows - count
        own_col = lax.broadcasted_iota(jnp.int32, (count, count), 1) + open_rows
        own_row = lax.broadcasted_iota(jnp.int32, (count, count), 0) + first_row
        causal = own_col <= own_row
        s0 = jnp.where(causal, scores_of(k0_ref[open_rows:own_rows, lanes]), low)
        s_open = scores_of(k0_ref[:open_rows, lanes]) if open_rows else None
        pick = lax.broadcasted_iota(jnp.int32, (seg_rows, HD), 0) < even * seg_rows
        s2 = scores_of(jnp.where(pick, k2e_ref[:, lanes], k2o_ref[:, lanes]))
        s1 = scores_of(k1_ref[:, lanes])
        if masked:
            col = lax.broadcasted_iota(jnp.int32, (count, seg_rows), 1)
            ok2 = col < jnp.where(seg >= 2, seg_rows, 0)
            ok1 = col < jnp.where(seg >= 1, seg_rows, 0)
            s2 = jnp.where(ok2, s2, low)
            s1 = jnp.where(ok1, s1, low)
        top = jnp.maximum(
            jnp.maximum(jnp.max(s2, axis=1, keepdims=True), jnp.max(s1, axis=1, keepdims=True)),
            jnp.max(s0, axis=1, keepdims=True),
        )
        if open_rows:
            top = jnp.maximum(top, jnp.max(s_open, axis=1, keepdims=True))
        e2 = jnp.exp(s2 - top)
        e1 = jnp.exp(s1 - top)
        if masked:
            e2 = jnp.where(ok2, e2, 0.0)
            e1 = jnp.where(ok1, e1, 0.0)
        e0 = jnp.where(causal, jnp.exp(s0 - top), 0.0)
        total = (
            jnp.sum(e2, axis=1, keepdims=True)
            + jnp.sum(e1, axis=1, keepdims=True)
            + jnp.sum(e0, axis=1, keepdims=True)
        )
        if open_rows:
            e_open = jnp.exp(s_open - top)
            total = total + jnp.sum(e_open, axis=1, keepdims=True)
        value2 = jnp.where(pick, v2e_ref[:, lanes], v2o_ref[:, lanes])
        mixed = jnp.dot(e2.astype(jnp.bfloat16), value2, preferred_element_type=jnp.float32)
        mixed = mixed + jnp.dot(e1.astype(jnp.bfloat16), v1_ref[:, lanes], preferred_element_type=jnp.float32)
        mixed = mixed + jnp.dot(
            e0.astype(jnp.bfloat16), v0_ref[open_rows:own_rows, lanes], preferred_element_type=jnp.float32
        )
        if open_rows:
            mixed = mixed + jnp.dot(
                e_open.astype(jnp.bfloat16), v0_ref[:open_rows, lanes], preferred_element_type=jnp.float32
            )
        o_ref[:, lanes] = (mixed / total).astype(o_ref.dtype)

    def run(masked, own_rows):
        for head in range(q_ref.shape[1] // HD):
            one_head(slice(head * HD, (head + 1) * HD), masked, own_rows)

    early = first_row + count <= count

    @pl.when(early)
    def _():
        run(True, count)

    @pl.when(jnp.logical_not(early))
    def _():
        run(True, seg_rows)


def attend(seg_number, first_row, query_rows, keys, values, head_lo, head_count):
    count = query_rows.shape[0]
    seg_rows = keys[0].shape[0]
    step = 1
    width = step * HD
    q_spec = pl.BlockSpec((count, width), lambda h, scalars: (0, h + head_lo // step))
    kv_spec = pl.BlockSpec((seg_rows, width), lambda h, scalars: (0, h + head_lo // step))
    even_spec = pl.BlockSpec((seg_rows, width), lambda h, scalars: (0, (h + head_lo // step) * scalars[2]))
    odd_spec = pl.BlockSpec((seg_rows, width), lambda h, scalars: (0, (h + head_lo // step) * (1 - scalars[2])))
    o_spec = pl.BlockSpec((count, width), lambda h, scalars: (0, h))
    mem_specs = [even_spec, odd_spec, kv_spec, kv_spec]
    grid_spec = pltpu.PrefetchScalarGridSpec(
        num_scalar_prefetch=1,
        grid=(head_count // step,),
        in_specs=[q_spec] + mem_specs + mem_specs,
        out_specs=o_spec,
    )
    even = (seg_number % 2 == 0).astype(jnp.int32)
    scalars = jnp.stack([seg_number, first_row, even]).astype(jnp.int32)
    return pl.pallas_call(
        attention_kernel,
        grid_spec=grid_spec,
        out_shape=jax.ShapeDtypeStruct((count, head_count * HD), jnp.bfloat16),
        interpret=INTERPRET,
    )(scalars, query_rows, *keys, *values)


def body(hidden_states, queries, w_key, w_value):
    tok_rows = hidden_states.shape[0]
    width = w_key.shape[1]
    halves = lax.axis_size("fsdp")
    segs = lax.axis_size("seg")
    cols = width // halves
    piece = cols // 8
    half_number = lax.axis_index("fsdp")
    seg_number = lax.axis_index("seg")
    other_half = 1 - half_number
    first_is_mine = half_number == 0
    core = seg_number % 2
    is_key_core = core == 0

    def mine_of(array):
        return lax.dynamic_slice_in_dim(array, half_number * cols, cols, 1)

    def theirs_of(array):
        return lax.dynamic_slice_in_dim(array, other_half * cols, cols, 1)

    served = jnp.where(is_key_core, theirs_of(w_key), theirs_of(w_value))
    left_got = swap_halves(served[:, :piece])
    stride = segs // 8 if segs >= 16 else 0
    wrap_pairs = []
    for seg in range(segs):
        for half in range(halves):
            wrap_pairs.append(((seg ^ stride) * halves + (1 - half), seg * halves + half))
    right_got = lax.ppermute(served[:, piece:], ("seg", "fsdp"), wrap_pairs)
    piece_got = jnp.concatenate([left_got, right_got], axis=1)
    core_pairs = [(seg, seg ^ 1) for seg in range(segs)]
    piece_other = lax.ppermute(piece_got, "seg", core_pairs)
    key_got = jnp.where(is_key_core, piece_got, piece_other)
    value_got = jnp.where(is_key_core, piece_other, piece_got)

    hidden_got = swap_halves(hidden_states)

    key_weights = in_order(first_is_mine, mine_of(w_key), key_got, 0)
    value_weights = in_order(first_is_mine, mine_of(w_value), value_got, 0)
    hidden_rows = in_order(first_is_mine, hidden_states, hidden_got, 0)

    own_key = jnp.dot(hidden_rows, key_weights, preferred_element_type=jnp.float32).astype(jnp.bfloat16)
    own_value = jnp.dot(hidden_rows, value_weights, preferred_element_type=jnp.float32).astype(
        jnp.bfloat16
    )
    query_sent, own_key, own_value = lax.optimization_barrier((theirs_of(queries), own_key, own_value))
    query_got = swap_halves(query_sent)

    even_pairs = [(s, s + 2) for s in range(0, segs - 2, 2)]
    forward_pairs = [(s, s + 1) for s in range(0, segs - 1, 2)]

    def shifted(own):
        one = from_behind(own, "seg", 1)
        even_two = lax.ppermute(own, "seg", even_pairs)
        odd_two = lax.ppermute(one, "seg", forward_pairs)
        return (even_two, odd_two), one

    key_one = from_behind(own_key, "seg", 1)
    value_one = from_behind(own_value, "seg", 1)
    both_two = lax.ppermute(jnp.stack([own_key, own_value]), "seg", even_pairs)
    key_two = (both_two[0], lax.ppermute(key_one, "seg", forward_pairs))
    value_two = (both_two[1], lax.ppermute(value_one, "seg", forward_pairs))
    keys = (*key_two, key_one, own_key)
    values = (*value_two, value_one, own_value)

    heads = cols // HD
    lead = heads - heads // 4
    mine_q = mine_of(queries)
    mine_lead = attend(seg_number, half_number * tok_rows, mine_q, keys, values, 0, lead)
    query_got, mine_lead = lax.optimization_barrier((query_got, mine_lead))
    got = []
    split = heads - 3 * heads // 8
    for head_lo, head_count in ((0, split), (split, heads - split)):
        their_rows = attend(seg_number, other_half * tok_rows, query_got, keys, values, head_lo, head_count)
        got.append(swap_halves(their_rows))
    mine_q, their_rows = lax.optimization_barrier((mine_q, their_rows))
    mine_tail = attend(seg_number, half_number * tok_rows, mine_q, keys, values, lead, heads - lead)
    mine_first = jnp.concatenate([mine_lead, mine_tail, *got], axis=1)
    theirs_first = jnp.concatenate([*got, mine_lead, mine_tail], axis=1)
    return jnp.where(first_is_mine, mine_first, theirs_first)


def solution(mesh):
    placed = (P(("seg", "fsdp"), None), P(("seg", "fsdp"), None), P("fsdp", None), P("fsdp", None))
    return jax.shard_map(
        body, mesh=mesh, in_specs=placed, out_specs=P(("seg", "fsdp"), None), check_vma=False
    )
```
